256 devices in a mesh: expert: 8 (over z), mp: 32 (over x, y, core).
Axes of the slice: x: 4, y: 4, z: 8, core: 2. Of those that a mesh axis runs over, the one named last changes fastest.
Arguments:
- tokens: bfloat16 [4096, 2048], P('expert', 'mp'), may hold values from -6 to 6
- expert_route: int32 [4096, 2], P('expert'), may hold values from 0 to 7, all different within a row; in each aligned block of 512 rows (0 to 511, 512 to 1023, ...) at most 256 rows name the same one
- route_gate: float32 [4096, 2], P('expert'), may hold values from 0.05 to 1
- request_lengths: int32 [32], replicated, may hold values from 1 to 1024, 4096 in all
- request_adapter: int32 [32], replicated, may hold values from 0 to 63, as said below
- request_order: int32 [32], replicated, may hold values from 0 to 31, each once
- gate_weight: bfloat16 [8, 5632, 2048], P('expert', 'mp'), may hold values from -0.125 to 0.125
- up_weight: bfloat16 [8, 5632, 2048], P('expert', 'mp'), may hold values from -0.125 to 0.125
- down_weight: bfloat16 [8, 5632, 2048], P('expert', 'mp'), may hold values from -0.15625 to 0.15625
- adapter_in: bfloat16 [8, 1024, 2048], P('expert', 'mp'), may hold values from -0.125 to 0.125
- adapter_out: bfloat16 [8, 5632, 1024], P('expert', 'mp'), may hold values from -1.5 to 1.5
Outputs:
- mixed: bfloat16 [4096, 2048], P('expert', 'mp')
The draws below stay inside these ranges and needn't reach their ends.
Inputs may be any that keep to these rules, and one draw needn't show every extreme that they name: `expert_route`: the two entries of a row differ; within each aligned block of 512 rows (the tokens held at one position along `expert`) no expert is named by more than 256 rows, and in some block some expert is named by exactly 256 rows. `request_lengths`: they sum to 4096; the largest is 1024. `request_order`: each request index appears once. `request_adapter`: exactly 16 different adapters appear.
All inputs are finite; a program needn't handle non-finite values.
Results may differ from the reference program's by a relative error of at most 0.035.
Values may be sent and summed in bfloat16 or wider, within the bound.
No kernel may reach another device: no remote copies, remote signals or barrier semaphores. Data moves between devices by JAX's collectives and lax.ppermute only.
A program may use at most 64 MiB of HBM per device.

```python
import math
import jax
import jax.numpy as jnp
import numpy as np
from jax import lax

D = 2048
FF = 5632
RANK = 16
ADAPTERS = 64
USED = 16
TOPK = 2
TOK_E = 512
EXPERTS = 8
CAP = 256
TOKENS = 4096
REQS = 32
MOST_LEN = 1024
N_EXPERT = 8
N_MP = 32


def draw_request_adapter(key, part):
    pool_key = jax.random.fold_in(key, 11)
    pick_key = jax.random.fold_in(key, 12)
    order_key = jax.random.fold_in(key, 13)
    middle = jax.random.permutation(pool_key, jnp.arange(1, ADAPTERS - 1, dtype=jnp.int32))[:USED - 2]
    ends_pair = jnp.array([0, ADAPTERS - 1], dtype=jnp.int32)
    adapter_pool = jnp.concatenate([ends_pair, middle.astype(jnp.int32)]).astype(jnp.int32)
    request_ids = jnp.arange(REQS, dtype=jnp.int32)
    assigned = jnp.where(request_ids < USED, request_ids, jax.random.randint(pick_key, (REQS,), 0, USED, dtype=jnp.int32))
    assigned = jax.random.permutation(order_key, assigned)
    return adapter_pool[assigned].astype(jnp.int32)


def raised(drawn, rng, source, target, shards_of, factor):
    def block_of(dim):
        return (jnp.arange(drawn.shape[dim]) // (drawn.shape[dim] // shards_of)).reshape((-1,) + (1,) * (drawn.ndim - 1 - dim))

    one_side = jax.random.permutation(rng, shards_of)[block_of(target)]
    other_side = (block_of(target) + shards_of // 2) % shards_of
    return jnp.where((block_of(source) == one_side) | (block_of(source) == other_side), factor * drawn, drawn)


def block_levels(key, extent, split, smallest, high):
    loudness = 1.0
    for position, blocks in split:
        heights = jax.random.uniform(jax.random.fold_in(jax.random.fold_in(key, 6), position), (blocks,), jnp.float32, smallest / len(split), high / len(split))
        loudness = loudness * jnp.repeat(jnp.exp(heights), extent[position] // blocks).reshape((-1,) + (1,) * (len(extent) - 1 - position))
    return loudness


def split_up(amount, total, reach, skew):
    loads = [(1 << 20) // math.isqrt(rank ** skew) + 1 for rank in range(2, amount + 1)]
    surplus, counts = total - reach - (amount - 1), [1] * (amount - 1)
    while surplus > 0:
        movable = [i for i in range(amount - 1) if counts[i] < reach]
        mass, left = sum([loads[i] for i in movable]), surplus
        for i in movable:
            more = min(reach - counts[i], max(1, left * loads[i] // mass), surplus)
            counts[i] = counts[i] + more
            surplus = surplus - more
    return np.array([reach] + counts)


def uneven(stream_key, amount, total, most, lean):
    if amount == 2:
        one = jax.random.randint(stream_key, (), max(1, total - most), min(most, total - 1) + 1)
        return jnp.stack([one, total - one])
    sizes = jnp.asarray(split_up(amount, total, most, lean), jnp.int32)
    twos = (amount - 1) // 2
    source_of, receiver = sizes[1:1 + 2 * twos:2], sizes[2:2 + 2 * twos:2]
    margin = jnp.minimum(source_of - 1, most - receiver)
    moved = jax.random.randint(jax.random.fold_in(stream_key, 1), (twos,), 0, 1 << 20) % (margin + 1)
    sizes = sizes.at[1:1 + 2 * twos:2].set(source_of - moved).at[2:2 + 2 * twos:2].set(receiver + moved)
    return sizes[jax.random.permutation(jax.random.fold_in(stream_key, 2), amount)]


def deal_out(own_key, own, number, rows, number_of, top, bound, lean):
    ranking = jax.random.permutation(own_key, number_of)
    packed, usual = portions_of(number_of, rows * top, bound, lean, True), portions_of(number_of, rows * top, bound, lean, False)
    places = jnp.arange(number_of)

    def named(sizes, rotation):
        used = int((sizes > 0).sum())
        fixed = max(1, used // 4)
        passed = fixed + (places - fixed + rotation * (used - fixed)) % max(1, number_of - fixed)
        return jnp.zeros((number_of,), jnp.int32).at[ranking[jnp.where(places < fixed, places, passed)]].set(jnp.asarray(sizes, jnp.int32))

    sizes = jnp.where(number % 4 == 0, named(packed, number // 4), named(usual, number - number // 4 - 1))
    mixed = jax.random.permutation(jax.random.fold_in(own, 3), number_of)
    source_of, taker = mixed[0:number_of // 2 * 2:2], mixed[1:number_of // 2 * 2:2]
    slack = jnp.minimum(sizes[source_of] - 1, bound - sizes[taker]) // 2
    slack = jnp.where((source_of == ranking[0]) | (taker == ranking[0]) | (sizes[taker] == 0), 0, jnp.maximum(slack, 0))
    passed = jax.random.randint(jax.random.fold_in(own, 4), (number_of // 2,), 0, 1 << 20) % (slack + 1)
    sizes = sizes.at[source_of].add(-passed).at[taker].add(passed)
    labels = jnp.searchsorted(jnp.cumsum(sizes), jnp.arange(rows * top), side="right").astype(jnp.int32)
    grid = labels.reshape(top, rows).T
    grid = grid[jax.random.permutation(jax.random.fold_in(own, 1), rows)]
    rotation = jax.random.randint(jax.random.fold_in(own, 2), (rows, 1), 0, top)
    return jnp.take_along_axis(grid, (jnp.arange(top)[None, :] + rotation) % top, axis=1)


def portions_of(count, total, bound, lean, full):
    portions = [(1 << 20) // math.isqrt(standing ** lean) + 1 for standing in range(1, count + 1)]
    largest = bound if full else min(bound, max(-(-total // count), total * portions[0] // sum(portions)))
    least = 1 if total - largest >= count - 1 else 0
    given, spare = [largest] + [least] * (count - 1), total - largest - least * (count - 1)
    while spare > 0:
        candidates = [i for i in range(1, count) if given[i] < largest] or [i for i in range(1, count) if given[i] < bound]
        mass, left = sum([portions[i] for i in candidates]), spare
        for i in candidates:
            addition = min(bound - given[i], max(1, left * portions[i] // mass), spare)
            given[i] = given[i] + addition
            spare = spare - addition
    return np.array(given)


def centred(rng, dims, width, most, cuts=(), held_as=jnp.bfloat16):
    values = jax.random.normal(rng, dims, jnp.float32) * width
    if len(cuts) > 0:
        values = block_levels(rng, dims, cuts, -0.22, 0.18) * values
    return jnp.clip(values, min=-most, max=most).astype(held_as)


def heavy_noise(key, extent, scale, reach, shards, heavy, kind=jnp.bfloat16):
    values = scale * jax.random.normal(key, extent, jnp.float32)
    if shards:
        values = values * block_levels(key, extent, shards, -0.22, 0.18)
    return jnp.clip(raised(values, jax.random.fold_in(key, 3), *heavy), -reach, reach).astype(kind)


def setup_inputs(seed: int = 0) -> dict:
    key_of = jax.random.split(jax.random.key(seed), 12)
    tokens = centred(key_of[0], (TOKENS, D), 1.0, 6.0, ((0, 8), (1, 32)))
    expert_route_keys = jax.random.split(jax.random.fold_in(key_of[1], 1), TOKENS // TOK_E)
    expert_route_turns = jax.random.permutation(jax.random.fold_in(key_of[1], 3), TOKENS // TOK_E)
    expert_route = jax.vmap(lambda own, number: deal_out(jax.random.fold_in(key_of[1], 2), own, number, TOK_E, EXPERTS, TOPK, CAP, 2))(expert_route_keys, expert_route_turns).reshape((TOKENS, TOPK))
    route_gate = jnp.clip(0.05 + 0.95 * jax.random.uniform(key_of[2], (TOKENS, TOPK), jnp.float32) ** block_levels(key_of[2], (TOKENS, TOPK), ((0, 8),), -0.2, 0.2), 0.05, 1.0)
    request_lengths = uneven(key_of[3], REQS, TOKENS, MOST_LEN, 2).astype(jnp.int32)
    request_adapter = draw_request_adapter(jax.random.fold_in(key_of[11], 71), 0)
    request_order = jax.random.permutation(key_of[5], REQS).astype(jnp.int32)
    gate_weight = centred(key_of[6], (EXPERTS, FF, D), D ** -0.5, 0.125, ((0, 8), (1, 32)))
    up_weight = centred(key_of[7], (EXPERTS, FF, D), D ** -0.5, 0.125, ((0, 8), (1, 32)))
    down_weight = heavy_noise(key_of[8], (EXPERTS, FF, D), FF ** -0.5, 0.15625, ((0, 8), (1, 32)), (1, 2, 32, 2.75))
    adapter_in = centred(key_of[9], (EXPERTS, ADAPTERS * RANK, D), D ** -0.5, 0.125, ((0, 8), (1, 32)))
    adapter_out = centred(key_of[10], (EXPERTS, FF, ADAPTERS * RANK), RANK ** -0.5, 1.5, ((0, 8), (1, 32)))
    return {"tokens": tokens, "expert_route": expert_route, "route_gate": route_gate, "request_lengths": request_lengths, "request_adapter": request_adapter, "request_order": request_order, "gate_weight": gate_weight, "up_weight": up_weight, "down_weight": down_weight, "adapter_in": adapter_in, "adapter_out": adapter_out}


def token_adapters(request_lengths, request_adapter, request_order, first_token, token_count):
    request_ids = jnp.arange(request_lengths.shape[0], dtype=jnp.int32)
    chosen = (request_order[:, None] == request_ids[None, :]).astype(jnp.int32)
    packed_lengths = jnp.sum(chosen * request_lengths[None, :], axis=1, dtype=jnp.int32)
    packed_adapters = jnp.sum(chosen * request_adapter[None, :], axis=1, dtype=jnp.int32)
    boundary = jnp.cumsum(packed_lengths, dtype=jnp.int32)
    positions = first_token + jnp.arange(token_count, dtype=jnp.int32)
    packed_index = jnp.sum((boundary[None, :] <= positions[:, None]).astype(jnp.int32), axis=1, dtype=jnp.int32)
    matches = (packed_index[:, None] == request_ids[None, :]).astype(jnp.int32)
    return jnp.sum(matches * packed_adapters[None, :], axis=1, dtype=jnp.int32)


def expert_slots(routes, groups, capacity):
    flat_routes = routes.reshape(-1)
    one_hot = (flat_routes[:, None] == jnp.arange(groups, dtype=jnp.int32)[None, :]).astype(jnp.int32)
    before = jnp.cumsum(one_hot, axis=0, dtype=jnp.int32) - one_hot
    seat_index = jnp.sum(before * one_hot, axis=1, dtype=jnp.int32)
    return (flat_routes * capacity + seat_index).reshape(routes.shape)


def contract_last(left, right):
    return lax.dot_general(left, right, (((1,), (1,)), ((), ())), preferred_element_type=jnp.float32)


def expert_block(operands):
    arrived, arrived_adapter, gate_w, up_w, down_w, rank_in, rank_out = operands
    row_count = arrived.shape[0]
    gate_pre = contract_last(arrived, gate_w)
    up_base = contract_last(arrived, up_w)
    rank_all = contract_last(arrived, rank_in)
    chosen = (arrived_adapter[:, None] == jnp.arange(ADAPTERS, dtype=jnp.int32)[None, :]).astype(jnp.float32)
    rank = jnp.sum(rank_all.reshape(row_count, ADAPTERS, RANK) * chosen[:, :, None], axis=1).astype(jnp.bfloat16)
    expanded = (rank[:, None, :] * chosen[:, :, None].astype(jnp.bfloat16)).reshape(row_count, ADAPTERS * RANK)
    up = up_base + contract_last(expanded, rank_out)
    hidden = (jax.nn.silu(gate_pre) * up).astype(jnp.bfloat16)
    block_width = FF // N_MP
    hidden_blocks = jnp.transpose(hidden.reshape(row_count, N_MP, block_width), (1, 0, 2))
    down_blocks = down_w.reshape(N_MP, block_width, D)

    def add_block(totals, pair):
        term = jnp.dot(pair[0], pair[1], preferred_element_type=jnp.float32)
        rounded = lax.optimization_barrier(term.astype(jnp.bfloat16))
        return totals + rounded.astype(jnp.float32), None

    summed, unused = lax.scan(add_block, jnp.zeros((row_count, D), jnp.float32), (hidden_blocks, down_blocks))
    return summed.astype(jnp.bfloat16)


def reference(tokens, expert_route, route_gate, request_lengths, request_adapter, request_order, gate_weight, up_weight, down_weight, adapter_in, adapter_out):
    adapter_of = token_adapters(request_lengths, request_adapter, request_order, 0, TOKENS)
    route_blocks = expert_route.reshape(N_EXPERT, TOK_E, TOPK)
    slots = jax.vmap(lambda block_routes: expert_slots(block_routes, EXPERTS, CAP))(route_blocks)
    seat_index = slots - route_blocks * CAP
    block_ids = jnp.arange(N_EXPERT, dtype=jnp.int32)[:, None, None]
    group_rows = N_EXPERT * CAP
    destination = (route_blocks * group_rows + block_ids * CAP + seat_index).reshape(TOKENS * TOPK)
    token_index = jnp.broadcast_to(jnp.arange(TOKENS, dtype=jnp.int32)[:, None], (TOKENS, TOPK)).reshape(TOKENS * TOPK)
    total_rows = EXPERTS * group_rows
    buffer = jnp.zeros((total_rows, D), jnp.bfloat16).at[destination].set(tokens[token_index])
    buffer_adapter = jnp.full((total_rows,), -1, jnp.int32).at[destination].set(adapter_of[token_index])
    outputs = lax.map(expert_block, (buffer.reshape(EXPERTS, group_rows, D), buffer_adapter.reshape(EXPERTS, group_rows), gate_weight, up_weight, down_weight, adapter_in, adapter_out))
    picked = outputs.reshape(total_rows, D)[destination].astype(jnp.float32).reshape(TOKENS, TOPK, D)
    mixed = jnp.sum(route_gate[:, :, None] * picked, axis=1)
    return mixed.astype(jnp.bfloat16)
```

```python
import jax
import jax.numpy as jnp
from jax import lax
from jax.sharding import PartitionSpec as P

RANK = 16
ADAPTERS = 64


def token_adapters(request_lengths, request_adapter, request_order, first_token, token_count):
    request_ids = jnp.arange(request_lengths.shape[0], dtype=jnp.int32)
    chosen = (request_order[:, None] == request_ids[None, :]).astype(jnp.int32)
    packed_lengths = jnp.sum(chosen * request_lengths[None, :], axis=1, dtype=jnp.int32)
    packed_adapters = jnp.sum(chosen * request_adapter[None, :], axis=1, dtype=jnp.int32)
    boundary = jnp.cumsum(packed_lengths, dtype=jnp.int32)
    positions = first_token + jnp.arange(token_count, dtype=jnp.int32)
    packed_index = jnp.sum(
        (boundary[None, :] <= positions[:, None]).astype(jnp.int32), axis=1, dtype=jnp.int32
    )
    matches = (packed_index[:, None] == request_ids[None, :]).astype(jnp.int32)
    return jnp.sum(matches * packed_adapters[None, :], axis=1, dtype=jnp.int32)


def expert_slots(routes, groups, capacity):
    flat_routes = routes.reshape(-1)
    one_hot = (flat_routes[:, None] == jnp.arange(groups, dtype=jnp.int32)[None, :]).astype(
        jnp.int32
    )
    before = jnp.cumsum(one_hot, axis=0, dtype=jnp.int32) - one_hot
    seat_index = jnp.sum(before * one_hot, axis=1, dtype=jnp.int32)
    return (flat_routes * capacity + seat_index).reshape(routes.shape)


def contract_last(left, right):
    return lax.dot_general(
        left, right, (((1,), (1,)), ((), ())), preferred_element_type=jnp.float32
    )


def on_device(
    tokens,
    expert_route,
    route_gate,
    request_lengths,
    request_adapter,
    request_order,
    gate_weight,
    up_weight,
    down_weight,
    adapter_in,
    adapter_out,
):
    tok_rows, local_feat = tokens.shape
    groups = lax.axis_size("expert")
    n_mp = lax.axis_size("mp")
    capacity = 4 * tok_rows // groups
    total_slots = groups * capacity
    source_group = lax.axis_index("expert")

    rank_w = adapter_in[0]
    rank_cols_w = lax.all_to_all(rank_w, "mp", split_axis=1, concat_axis=0, tiled=True)

    adapter_of = token_adapters(
        request_lengths, request_adapter, request_order, source_group * tok_rows, tok_rows
    )
    slot_index = expert_slots(expert_route, groups, capacity)
    flat_slots = slot_index.reshape(-1)
    flat_tokens = jnp.broadcast_to(
        jnp.arange(tok_rows, dtype=jnp.int32)[:, None], slot_index.shape
    ).reshape(-1)
    slot_token = jnp.zeros((total_slots,), jnp.int32).at[flat_slots].set(flat_tokens)
    filled = jnp.zeros((total_slots,), jnp.bool_).at[flat_slots].set(True)
    slot_adapter = jnp.where(filled, adapter_of[slot_token], -1)
    blank = jnp.zeros((), tokens.dtype)
    send_rows = jnp.where(filled[:, None], tokens[slot_token], blank)
    arrived_local = lax.all_to_all(send_rows, "expert", split_axis=0, concat_axis=0, tiled=True)
    arrived_adapter = lax.all_to_all(slot_adapter, "expert", split_axis=0, concat_axis=0, tiled=True)
    row_count = arrived_local.shape[0]

    part_all = contract_last(arrived_local, rank_cols_w)
    pick = (arrived_adapter[:, None] == jnp.arange(ADAPTERS, dtype=jnp.int32)[None, :]).astype(
        jnp.float32
    )
    part_rank = jnp.sum(part_all.reshape(row_count, ADAPTERS, RANK) * pick[:, :, None], axis=1)

    arrived = lax.all_gather(arrived_local, "mp", axis=1, tiled=True)
    parts = lax.all_gather(part_rank.astype(jnp.bfloat16), "mp", axis=0, tiled=False)
    rank = jnp.sum(parts.astype(jnp.float32), axis=0).astype(jnp.bfloat16)

    gate_pre = contract_last(arrived, gate_weight[0])
    up_base = contract_last(arrived, up_weight[0])
    chosen = pick.astype(jnp.bfloat16)
    expanded = (rank[:, None, :] * chosen[:, :, None]).reshape(row_count, ADAPTERS * RANK)
    up = up_base + contract_last(expanded, adapter_out[0])
    hidden = (jax.nn.silu(gate_pre) * up).astype(jnp.bfloat16)
    down_w = down_weight[0]
    scattered = lax.psum_scatter(
        lax.dot_general(
            down_w, hidden, (((0,), (1,)), ((), ())), preferred_element_type=jnp.float32
        ).astype(jnp.bfloat16),
        "mp",
        scatter_dimension=0,
        tiled=True,
    )
    returned = lax.all_to_all(scattered, "expert", split_axis=1, concat_axis=1, tiled=True)
    returned_rows = jnp.transpose(returned)
    picked = returned_rows[slot_index].astype(jnp.float32)
    mixed = jnp.sum(route_gate[:, :, None] * picked, axis=1)
    return mixed.astype(jnp.bfloat16)


def solution(mesh):
    in_specs = (
        P("expert", "mp"),
        P("expert", None),
        P("expert", None),
        P(),
        P(),
        P(),
        P("expert", "mp", None),
        P("expert", "mp", None),
        P("expert", "mp", None),
        P("expert", "mp", None),
        P("expert", "mp", None),
    )
    out_specs = P("expert", "mp")
    return jax.shard_map(
        on_device, mesh=mesh, in_specs=in_specs, out_specs=out_specs, check_vma=False
    )
```

```python
import jax
import jax.numpy as jnp
from jax import lax
from jax.sharding import PartitionSpec as P

RANK = 16
ADAPTERS = 64


def token_adapters(request_lengths, request_adapter, request_order, first_token, token_count):
    request_ids = jnp.arange(request_lengths.shape[0], dtype=jnp.int32)
    chosen = (request_order[:, None] == request_ids[None, :]).astype(jnp.int32)
    packed_lengths = jnp.sum(chosen * request_lengths[None, :], axis=1, dtype=jnp.int32)
    packed_adapters = jnp.sum(chosen * request_adapter[None, :], axis=1, dtype=jnp.int32)
    boundary = jnp.cumsum(packed_lengths, dtype=jnp.int32)
    positions = first_token + jnp.arange(token_count, dtype=jnp.int32)
    packed_index = jnp.sum(
        (boundary[None, :] <= positions[:, None]).astype(jnp.int32), axis=1, dtype=jnp.int32
    )
    matches = (packed_index[:, None] == request_ids[None, :]).astype(jnp.int32)
    return jnp.sum(matches * packed_adapters[None, :], axis=1, dtype=jnp.int32)


def expert_slots(routes, groups, capacity):
    flat_routes = routes.reshape(-1)
    one_hot = (flat_routes[:, None] == jnp.arange(groups, dtype=jnp.int32)[None, :]).astype(
        jnp.int32
    )
    before = jnp.cumsum(one_hot, axis=0, dtype=jnp.int32) - one_hot
    seat_index = jnp.sum(before * one_hot, axis=1, dtype=jnp.int32)
    return (flat_routes * capacity + seat_index).reshape(routes.shape)


def contract_last(left, right):
    return lax.dot_general(
        left, right, (((1,), (1,)), ((), ())), preferred_element_type=jnp.float32
    )


def on_device(
    tokens,
    expert_route,
    route_gate,
    request_lengths,
    request_adapter,
    request_order,
    gate_weight,
    up_weight,
    down_weight,
    adapter_in,
    adapter_out,
):
    tok_rows, local_feat = tokens.shape
    groups = lax.axis_size("expert")
    n_mp = lax.axis_size("mp")
    capacity = 4 * tok_rows // groups
    total_slots = groups * capacity
    source_group = lax.axis_index("expert")

    rank_w = adapter_in[0]
    rank_cols_w = lax.all_to_all(rank_w, "mp", split_axis=1, concat_axis=0, tiled=True)

    adapter_of = token_adapters(
        request_lengths, request_adapter, request_order, source_group * tok_rows, tok_rows
    )
    slot_index = expert_slots(expert_route, groups, capacity)
    slot_ids = jnp.arange(total_slots, dtype=jnp.int32)[:, None]
    seat = (
        (slot_index[None, :, 0] == slot_ids) | (slot_index[None, :, 1] == slot_ids)
    ).astype(tokens.dtype)
    send_rows = jnp.dot(seat, tokens, preferred_element_type=jnp.float32).astype(tokens.dtype)
    id_plus = jnp.dot(
        seat, (adapter_of + 1).astype(tokens.dtype), preferred_element_type=jnp.float32
    ) - 1.0
    payload = jnp.concatenate(
        [
            send_rows.reshape(groups, capacity, local_feat),
            id_plus.astype(tokens.dtype).reshape(groups, capacity // local_feat, local_feat),
        ],
        axis=1,
    )
    chunk = payload.shape[1]
    received = lax.all_to_all(
        payload.reshape(groups * chunk, local_feat), "expert", split_axis=0, concat_axis=0, tiled=True
    ).reshape(groups, chunk, local_feat)
    arrived_local = received[:, :capacity].reshape(total_slots, local_feat)
    arrived_adapter = received[:, capacity:].reshape(total_slots).astype(jnp.int32)
    row_count = arrived_local.shape[0]

    part_all = contract_last(arrived_local, rank_cols_w)
    pick = (arrived_adapter[:, None] == jnp.arange(ADAPTERS, dtype=jnp.int32)[None, :]).astype(
        jnp.float32
    )
    part_rank = jnp.sum(part_all.reshape(row_count, ADAPTERS, RANK) * pick[:, :, None], axis=1)
    part_rows = row_count * RANK // local_feat
    payload2 = jnp.concatenate(
        [arrived_local, part_rank.astype(tokens.dtype).reshape(part_rows, local_feat)], axis=0
    )
    gathered = lax.all_gather(payload2, "mp", axis=1, tiled=True)
    arrived = gathered[:row_count]
    rank = (
        jnp.sum(
            gathered[row_count:].reshape(part_rows, n_mp, local_feat).astype(jnp.float32), axis=1
        )
        .reshape(row_count, RANK)
        .astype(jnp.bfloat16)
    )

    gate_pre = contract_last(arrived, gate_weight[0])
    up_base = contract_last(arrived, up_weight[0])
    chosen = pick.astype(jnp.bfloat16)
    expanded = (rank[:, None, :] * chosen[:, :, None]).reshape(row_count, ADAPTERS * RANK)
    up = up_base + contract_last(expanded, adapter_out[0])
    hidden = (jax.nn.silu(gate_pre) * up).astype(jnp.bfloat16)
    down_w = down_weight[0]
    scattered = lax.psum_scatter(
        lax.dot_general(
            down_w, hidden, (((0,), (1,)), ((), ())), preferred_element_type=jnp.float32
        ).astype(jnp.bfloat16),
        "mp",
        scatter_dimension=0,
        tiled=True,
    )
    returned = lax.all_to_all(scattered, "expert", split_axis=1, concat_axis=1, tiled=True)
    returned_rows = jnp.transpose(returned)
    picked = returned_rows[slot_index].astype(jnp.float32)
    mixed = jnp.sum(route_gate[:, :, None] * picked, axis=1)
    return mixed.astype(jnp.bfloat16)


def solution(mesh):
    in_specs = (
        P("expert", "mp"),
        P("expert", None),
        P("expert", None),
        P(),
        P(),
        P(),
        P("expert", "mp", None),
        P("expert", "mp", None),
        P("expert", "mp", None),
        P("expert", "mp", None),
        P("expert", "mp", None),
    )
    out_specs = P("expert", "mp")
    return jax.shard_map(
        on_device, mesh=mesh, in_specs=in_specs, out_specs=out_specs, check_vma=False
    )
```

```python
import jax
import jax.numpy as jnp
from jax import lax
from jax.sharding import PartitionSpec as P

RANK = 16
ADAPTERS = 64


def token_adapters(request_lengths, request_adapter, request_order, first_token, token_count):
    request_ids = jnp.arange(request_lengths.shape[0], dtype=jnp.int32)
    chosen = (request_order[:, None] == request_ids[None, :]).astype(jnp.int32)
    packed_lengths = jnp.sum(chosen * request_lengths[None, :], axis=1, dtype=jnp.int32)
    packed_adapters = jnp.sum(chosen * request_adapter[None, :], axis=1, dtype=jnp.int32)
    boundary = jnp.cumsum(packed_lengths, dtype=jnp.int32)
    positions = first_token + jnp.arange(token_count, dtype=jnp.int32)
    packed_index = jnp.sum(
        (boundary[None, :] <= positions[:, None]).astype(jnp.int32), axis=1, dtype=jnp.int32
    )
    matches = (packed_index[:, None] == request_ids[None, :]).astype(jnp.int32)
    return jnp.sum(matches * packed_adapters[None, :], axis=1, dtype=jnp.int32)


def expert_slots(routes, groups, capacity):
    flat_routes = routes.reshape(-1)
    one_hot = (flat_routes[:, None] == jnp.arange(groups, dtype=jnp.int32)[None, :]).astype(
        jnp.int32
    )
    before = jnp.cumsum(one_hot, axis=0, dtype=jnp.int32) - one_hot
    seat_index = jnp.sum(before * one_hot, axis=1, dtype=jnp.int32)
    return (flat_routes * capacity + seat_index).reshape(routes.shape)


def contract_last(left, right):
    return lax.dot_general(
        left, right, (((1,), (1,)), ((), ())), preferred_element_type=jnp.float32
    )


def on_device(
    tokens,
    expert_route,
    route_gate,
    request_lengths,
    request_adapter,
    request_order,
    gate_weight,
    up_weight,
    down_weight,
    adapter_in,
    adapter_out,
):
    tok_rows, local_feat = tokens.shape
    groups = lax.axis_size("expert")
    n_mp = lax.axis_size("mp")
    capacity = 4 * tok_rows // groups
    total_slots = groups * capacity
    source_group = lax.axis_index("expert")

    rank_w = adapter_in[0]
    rank_cols_w = lax.all_to_all(rank_w, "mp", split_axis=1, concat_axis=0, tiled=True)
    down_cols_w = lax.all_to_all(down_weight[0], "mp", split_axis=1, concat_axis=0, tiled=True)

    adapter_of = token_adapters(
        request_lengths, request_adapter, request_order, source_group * tok_rows, tok_rows
    )
    slot_index = expert_slots(expert_route, groups, capacity)
    slot_ids = jnp.arange(total_slots, dtype=jnp.int32)[:, None]
    seat = (
        (slot_index[None, :, 0] == slot_ids) | (slot_index[None, :, 1] == slot_ids)
    ).astype(tokens.dtype)
    send_rows = jnp.dot(seat, tokens, preferred_element_type=jnp.float32).astype(tokens.dtype)
    id_plus = jnp.dot(
        seat, (adapter_of + 1).astype(tokens.dtype), preferred_element_type=jnp.float32
    ) - 1.0
    payload = jnp.concatenate(
        [
            send_rows.reshape(groups, capacity, local_feat),
            id_plus.astype(tokens.dtype).reshape(groups, capacity // local_feat, local_feat),
        ],
        axis=1,
    )
    chunk = payload.shape[1]
    received = lax.all_to_all(
        payload.reshape(groups * chunk, local_feat), "expert", split_axis=0, concat_axis=0, tiled=True
    ).reshape(groups, chunk, local_feat)
    arrived_local = received[:, :capacity].reshape(total_slots, local_feat)
    arrived_adapter = received[:, capacity:].reshape(total_slots).astype(jnp.int32)
    row_count = arrived_local.shape[0]

    part_all = contract_last(arrived_local, rank_cols_w)
    pick = (arrived_adapter[:, None] == jnp.arange(ADAPTERS, dtype=jnp.int32)[None, :]).astype(
        jnp.float32
    )
    part_rank = jnp.sum(part_all.reshape(row_count, ADAPTERS, RANK) * pick[:, :, None], axis=1)
    part_rows = row_count * RANK // local_feat
    payload2 = jnp.concatenate(
        [arrived_local, part_rank.astype(tokens.dtype).reshape(part_rows, local_feat)], axis=0
    )
    gathered = lax.all_gather(payload2, "mp", axis=1, tiled=True)
    arrived = gathered[:row_count]
    rank = (
        jnp.sum(
            gathered[row_count:].reshape(part_rows, n_mp, local_feat).astype(jnp.float32), axis=1
        )
        .reshape(row_count, RANK)
        .astype(jnp.bfloat16)
    )

    gate_pre = contract_last(arrived, gate_weight[0])
    up_base = contract_last(arrived, up_weight[0])
    chosen = pick.astype(jnp.bfloat16)
    expanded = (rank[:, None, :] * chosen[:, :, None]).reshape(row_count, ADAPTERS * RANK)
    up = up_base + contract_last(expanded, adapter_out[0])
    hidden = (jax.nn.silu(gate_pre) * up).astype(jnp.bfloat16)
    hidden_full = lax.all_gather(hidden, "mp", axis=1, tiled=True)
    down_local = jnp.dot(hidden_full, down_cols_w, preferred_element_type=jnp.float32).astype(
        jnp.bfloat16
    )
    returned_rows = lax.all_to_all(down_local, "expert", split_axis=0, concat_axis=0, tiled=True)
    picked = returned_rows[slot_index].astype(jnp.float32)
    mixed = jnp.sum(route_gate[:, :, None] * picked, axis=1)
    return mixed.astype(jnp.bfloat16)


def solution(mesh):
    in_specs = (
        P("expert", "mp"),
        P("expert", None),
        P("expert", None),
        P(),
        P(),
        P(),
        P("expert", "mp", None),
        P("expert", "mp", None),
        P("expert", "mp", None),
        P("expert", "mp", None),
        P("expert", "mp", None),
    )
    out_specs = P("expert", "mp")
    return jax.shard_map(
        on_device, mesh=mesh, in_specs=in_specs, out_specs=out_specs, check_vma=False
    )
```

```python
import jax
import jax.numpy as jnp
from jax import lax
from jax.sharding import PartitionSpec as P

RANK = 16
ADAPTERS = 64


def token_adapters(request_lengths, request_adapter, request_order, first_token, token_count):
    request_ids = jnp.arange(request_lengths.shape[0], dtype=jnp.int32)
    chosen = (request_order[:, None] == request_ids[None, :]).astype(jnp.int32)
    packed_lengths = jnp.sum(chosen * request_lengths[None, :], axis=1, dtype=jnp.int32)
    packed_adapters = jnp.sum(chosen * request_adapter[None, :], axis=1, dtype=jnp.int32)
    boundary = jnp.cumsum(packed_lengths, dtype=jnp.int32)
    positions = first_token + jnp.arange(token_count, dtype=jnp.int32)
    packed_index = jnp.sum(
        (boundary[None, :] <= positions[:, None]).astype(jnp.int32), axis=1, dtype=jnp.int32
    )
    matches = (packed_index[:, None] == request_ids[None, :]).astype(jnp.int32)
    return jnp.sum(matches * packed_adapters[None, :], axis=1, dtype=jnp.int32)


def expert_slots(routes, groups, capacity):
    flat_routes = routes.reshape(-1)
    one_hot = (flat_routes[:, None] == jnp.arange(groups, dtype=jnp.int32)[None, :]).astype(
        jnp.int32
    )
    before = jnp.cumsum(one_hot, axis=0, dtype=jnp.int32) - one_hot
    seat_index = jnp.sum(before * one_hot, axis=1, dtype=jnp.int32)
    return (flat_routes * capacity + seat_index).reshape(routes.shape)


def contract_last(left, right):
    return lax.dot_general(
        left, right, (((1,), (1,)), ((), ())), preferred_element_type=jnp.float32
    )


def on_device(
    tokens,
    expert_route,
    route_gate,
    request_lengths,
    request_adapter,
    request_order,
    gate_weight,
    up_weight,
    down_weight,
    adapter_in,
    adapter_out,
):
    tok_rows, local_feat = tokens.shape
    width = gate_weight.shape[2]
    lora_width = adapter_out.shape[2]
    groups = lax.axis_size("expert")
    n_chip = lax.axis_size("chip")
    n_core = lax.axis_size("core")
    n_mp = n_chip * n_core
    capacity = 4 * tok_rows // groups
    total_slots = groups * capacity
    half = total_slots // n_core
    core = lax.axis_index("core")
    source_group = lax.axis_index("expert")

    rank_cols_w = lax.all_to_all(
        adapter_in[0], ("chip", "core"), split_axis=1, concat_axis=0, tiled=True
    )
    own_w = jnp.concatenate([gate_weight[0], up_weight[0], down_weight[0], adapter_out[0]], axis=1)
    partner_w = lax.ppermute(own_w, "core", [(0, 1), (1, 0)])
    pair_w = jnp.concatenate([own_w, partner_w], axis=0)
    down_cols_w = lax.all_to_all(
        pair_w[:, 2 * width : 3 * width], "chip", split_axis=1, concat_axis=0, tiled=True
    )

    adapter_of = token_adapters(
        request_lengths, request_adapter, request_order, source_group * tok_rows, tok_rows
    )
    slot_index = expert_slots(expert_route, groups, capacity)
    slot_ids = jnp.arange(total_slots, dtype=jnp.int32)[:, None]
    seat = (
        (slot_index[None, :, 0] == slot_ids) | (slot_index[None, :, 1] == slot_ids)
    ).astype(tokens.dtype)
    send_rows = jnp.dot(seat, tokens, preferred_element_type=jnp.float32).astype(tokens.dtype)
    id_plus = jnp.dot(
        seat, (adapter_of + 1).astype(tokens.dtype), preferred_element_type=jnp.float32
    ) - 1.0
    payload = jnp.concatenate(
        [
            send_rows.reshape(groups, capacity, local_feat),
            id_plus.astype(tokens.dtype).reshape(groups, capacity // local_feat, local_feat),
        ],
        axis=1,
    )
    chunk = payload.shape[1]
    received = lax.all_to_all(
        payload.reshape(groups * chunk, local_feat), "expert", split_axis=0, concat_axis=0, tiled=True
    ).reshape(groups, chunk, local_feat)
    arrived_local = received[:, :capacity].reshape(total_slots, local_feat)
    arrived_adapter = received[:, capacity:].reshape(total_slots).astype(jnp.int32)
    row_count = arrived_local.shape[0]

    part_all = contract_last(arrived_local, rank_cols_w)
    pick = (arrived_adapter[:, None] == jnp.arange(ADAPTERS, dtype=jnp.int32)[None, :]).astype(
        jnp.float32
    )
    part_rank = jnp.sum(part_all.reshape(row_count, ADAPTERS, RANK) * pick[:, :, None], axis=1)
    part_rows = row_count * RANK // local_feat
    halves = jnp.concatenate(
        [
            arrived_local.reshape(n_core, half, local_feat),
            part_rank.astype(tokens.dtype).reshape(n_core, part_rows // n_core, local_feat),
        ],
        axis=1,
    )
    swapped = lax.all_to_all(halves, "core", split_axis=0, concat_axis=0, tiled=True)
    pair_rows = jnp.transpose(swapped, (1, 0, 2)).reshape(swapped.shape[1], n_core * local_feat)
    gathered = lax.all_gather(pair_rows, "chip", axis=1, tiled=True)
    arrived = gathered[:half]
    rank_rows = part_rows // n_core
    rank = (
        jnp.sum(gathered[half:].reshape(rank_rows, n_mp, local_feat).astype(jnp.float32), axis=1)
        .reshape(half, RANK)
        .astype(jnp.bfloat16)
    )
    half_adapter = lax.dynamic_slice_in_dim(arrived_adapter, core * half, half)
    chosen = (half_adapter[:, None] == jnp.arange(ADAPTERS, dtype=jnp.int32)[None, :]).astype(
        jnp.bfloat16
    )

    gate_pre = contract_last(arrived, pair_w[:, :width])
    up_base = contract_last(arrived, pair_w[:, width : 2 * width])
    expanded = (rank[:, None, :] * chosen[:, :, None]).reshape(half, ADAPTERS * RANK)
    up = up_base + contract_last(expanded, pair_w[:, 3 * width : 3 * width + lora_width])
    hidden = (jax.nn.silu(gate_pre) * up).astype(jnp.bfloat16)
    hidden_full = lax.all_gather(hidden, "chip", axis=1, tiled=True)
    down_pair = jnp.dot(hidden_full, down_cols_w, preferred_element_type=jnp.float32).astype(
        jnp.bfloat16
    )
    down_local = lax.all_to_all(
        down_pair.reshape(half, n_core, local_feat), "core", split_axis=1, concat_axis=0, tiled=True
    ).reshape(total_slots, local_feat)
    returned_rows = lax.all_to_all(down_local, "expert", split_axis=0, concat_axis=0, tiled=True)
    picked = returned_rows[slot_index].astype(jnp.float32)
    mixed = jnp.sum(route_gate[:, :, None] * picked, axis=1)
    return mixed.astype(jnp.bfloat16)


def solution(mesh):
    n_expert, n_mp = mesh.devices.shape
    split = jax.sharding.Mesh(
        mesh.devices.reshape(n_expert, n_mp // 2, 2), ("expert", "chip", "core")
    )
    mp = ("chip", "core")
    in_specs = (
        P("expert", mp),
        P("expert", None),
        P("expert", None),
        P(),
        P(),
        P(),
        P("expert", mp, None),
        P("expert", mp, None),
        P("expert", mp, None),
        P("expert", mp, None),
        P("expert", mp, None),
    )
    out_specs = P("expert", mp)
    return jax.shard_map(
        on_device, mesh=split, in_specs=in_specs, out_specs=out_specs, check_vma=False
    )
```

```python
import jax
import jax.numpy as jnp
from jax import lax
from jax.sharding import PartitionSpec as P

RANK = 16
ADAPTERS = 64


def token_adapters(request_lengths, request_adapter, request_order, first_token, token_count):
    request_ids = jnp.arange(request_lengths.shape[0], dtype=jnp.int32)
    chosen = (request_order[:, None] == request_ids[None, :]).astype(jnp.int32)
    packed_lengths = jnp.sum(chosen * request_lengths[None, :], axis=1, dtype=jnp.int32)
    packed_adapters = jnp.sum(chosen * request_adapter[None, :], axis=1, dtype=jnp.int32)
    boundary = jnp.cumsum(packed_lengths, dtype=jnp.int32)
    positions = first_token + jnp.arange(token_count, dtype=jnp.int32)
    packed_index = jnp.sum(
        (boundary[None, :] <= positions[:, None]).astype(jnp.int32), axis=1, dtype=jnp.int32
    )
    matches = (packed_index[:, None] == request_ids[None, :]).astype(jnp.int32)
    return jnp.sum(matches * packed_adapters[None, :], axis=1, dtype=jnp.int32)


def expert_slots(routes, groups, capacity):
    flat_routes = routes.reshape(-1)
    one_hot = (flat_routes[:, None] == jnp.arange(groups, dtype=jnp.int32)[None, :]).astype(
        jnp.int32
    )
    before = jnp.cumsum(one_hot, axis=0, dtype=jnp.int32) - one_hot
    seat_index = jnp.sum(before * one_hot, axis=1, dtype=jnp.int32)
    return (flat_routes * capacity + seat_index).reshape(routes.shape)


def contract_last(left, right):
    return lax.dot_general(
        left, right, (((1,), (1,)), ((), ())), preferred_element_type=jnp.float32
    )


def on_device(
    tokens,
    expert_route,
    route_gate,
    request_lengths,
    request_adapter,
    request_order,
    gate_weight,
    up_weight,
    down_weight,
    adapter_in,
    adapter_out,
):
    tok_rows, local_feat = tokens.shape
    width = gate_weight.shape[2]
    lora_width = adapter_out.shape[2]
    groups = lax.axis_size("expert")
    n_chip = lax.axis_size("chip")
    n_core = lax.axis_size("core")
    n_mp = n_chip * n_core
    capacity = 4 * tok_rows // groups
    total_slots = groups * capacity
    half = total_slots // n_core
    core = lax.axis_index("core")
    source_group = lax.axis_index("expert")

    rank_cols_w = lax.all_to_all(
        adapter_in[0], ("chip", "core"), split_axis=1, concat_axis=0, tiled=True
    )
    own_w = jnp.concatenate([gate_weight[0], up_weight[0], down_weight[0], adapter_out[0]], axis=1)
    partner_w = lax.ppermute(own_w, "core", [(0, 1), (1, 0)])
    pair_w = jnp.concatenate([own_w, partner_w], axis=0)
    down_cols_w = lax.all_to_all(
        pair_w[:, 2 * width : 3 * width], "chip", split_axis=1, concat_axis=0, tiled=True
    )

    adapter_of = token_adapters(
        request_lengths, request_adapter, request_order, source_group * tok_rows, tok_rows
    )
    slot_index = expert_slots(expert_route, groups, capacity)
    slot_ids = jnp.arange(total_slots, dtype=jnp.int32)[:, None]
    seat = (
        (slot_index[None, :, 0] == slot_ids) | (slot_index[None, :, 1] == slot_ids)
    ).astype(tokens.dtype)
    send_rows = jnp.dot(seat, tokens, preferred_element_type=jnp.float32).astype(tokens.dtype)
    id_plus = jnp.dot(
        seat, (adapter_of + 1).astype(tokens.dtype), preferred_element_type=jnp.float32
    ) - 1.0
    payload = jnp.concatenate(
        [
            send_rows.reshape(groups, capacity, local_feat),
            id_plus.astype(tokens.dtype).reshape(groups, capacity // local_feat, local_feat),
        ],
        axis=1,
    )
    chunk = payload.shape[1]
    received = lax.all_to_all(
        payload.reshape(groups * chunk, local_feat), "expert", split_axis=0, concat_axis=0, tiled=True
    ).reshape(groups, chunk, local_feat)
    arrived_local = received[:, :capacity].reshape(total_slots, local_feat)
    arrived_adapter = received[:, capacity:].reshape(total_slots).astype(jnp.int32)
    row_count = arrived_local.shape[0]

    part_all = contract_last(arrived_local, rank_cols_w)
    pick = (arrived_adapter[:, None] == jnp.arange(ADAPTERS, dtype=jnp.int32)[None, :]).astype(
        jnp.float32
    )
    part_rank = jnp.sum(part_all.reshape(row_count, ADAPTERS, RANK) * pick[:, :, None], axis=1)
    part_rows = row_count * RANK // local_feat
    halves = jnp.concatenate(
        [
            arrived_local.reshape(n_core, half, local_feat),
            part_rank.astype(tokens.dtype).reshape(n_core, part_rows // n_core, local_feat),
        ],
        axis=1,
    )
    swapped = lax.all_to_all(halves, "core", split_axis=0, concat_axis=0, tiled=True)
    pair_rows = jnp.transpose(swapped, (1, 0, 2)).reshape(swapped.shape[1], n_core * local_feat)
    gathered = lax.all_gather(pair_rows, "chip", axis=1, tiled=True)
    arrived = gathered[:half]
    rank_rows = part_rows // n_core
    rank = (
        jnp.sum(gathered[half:].reshape(rank_rows, n_mp, local_feat).astype(jnp.float32), axis=1)
        .reshape(half, RANK)
        .astype(jnp.bfloat16)
    )
    half_adapter = lax.dynamic_slice_in_dim(arrived_adapter, core * half, half)
    chosen = (half_adapter[:, None] == jnp.arange(ADAPTERS, dtype=jnp.int32)[None, :]).astype(
        jnp.bfloat16
    )

    gate_pre = contract_last(pair_w[:, :width], arrived)
    up_base = contract_last(pair_w[:, width : 2 * width], arrived)
    expanded = (rank[:, None, :] * chosen[:, :, None]).reshape(half, ADAPTERS * RANK)
    up = up_base + contract_last(pair_w[:, 3 * width : 3 * width + lora_width], expanded)
    hidden = (jax.nn.silu(gate_pre) * up).astype(jnp.bfloat16)
    hidden_full = lax.all_gather(hidden, "chip", axis=0, tiled=True)
    down_pair = lax.dot_general(
        hidden_full, down_cols_w, (((0,), (0,)), ((), ())), preferred_element_type=jnp.float32
    ).astype(jnp.bfloat16)
    down_local = lax.all_to_all(
        down_pair.reshape(half, n_core, local_feat), "core", split_axis=1, concat_axis=0, tiled=True
    ).reshape(total_slots, local_feat)
    returned_rows = lax.all_to_all(down_local, "expert", split_axis=0, concat_axis=0, tiled=True)
    picked = returned_rows[slot_index].astype(jnp.float32)
    mixed = jnp.sum(route_gate[:, :, None] * picked, axis=1)
    return mixed.astype(jnp.bfloat16)


def solution(mesh):
    n_expert, n_mp = mesh.devices.shape
    split = jax.sharding.Mesh(
        mesh.devices.reshape(n_expert, n_mp // 2, 2), ("expert", "chip", "core")
    )
    mp = ("chip", "core")
    in_specs = (
        P("expert", mp),
        P("expert", None),
        P("expert", None),
        P(),
        P(),
        P(),
        P("expert", mp, None),
        P("expert", mp, None),
        P("expert", mp, None),
        P("expert", mp, None),
        P("expert", mp, None),
    )
    out_specs = P("expert", mp)
    return jax.shard_map(
        on_device, mesh=split, in_specs=in_specs, out_specs=out_specs, check_vma=False
    )
```

```python
import jax
import jax.numpy as jnp
from jax import lax
from jax.sharding import PartitionSpec as P

RANK = 16
ADAPTERS = 64


def token_adapters(request_lengths, request_adapter, request_order, first_token, token_count):
    request_ids = jnp.arange(request_lengths.shape[0], dtype=jnp.int32)
    chosen = (request_order[:, None] == request_ids[None, :]).astype(jnp.int32)
    packed_lengths = jnp.sum(chosen * request_lengths[None, :], axis=1, dtype=jnp.int32)
    packed_adapters = jnp.sum(chosen * request_adapter[None, :], axis=1, dtype=jnp.int32)
    boundary = jnp.cumsum(packed_lengths, dtype=jnp.int32)
    positions = first_token + jnp.arange(token_count, dtype=jnp.int32)
    packed_index = jnp.sum(
        (boundary[None, :] <= positions[:, None]).astype(jnp.int32), axis=1, dtype=jnp.int32
    )
    matches = (packed_index[:, None] == request_ids[None, :]).astype(jnp.int32)
    return jnp.sum(matches * packed_adapters[None, :], axis=1, dtype=jnp.int32)


def expert_slots(routes, groups, capacity):
    flat_routes = routes.reshape(-1)
    one_hot = (flat_routes[:, None] == jnp.arange(groups, dtype=jnp.int32)[None, :]).astype(
        jnp.int32
    )
    before = jnp.cumsum(one_hot, axis=0, dtype=jnp.int32) - one_hot
    seat_index = jnp.sum(before * one_hot, axis=1, dtype=jnp.int32)
    return (flat_routes * capacity + seat_index).reshape(routes.shape)


def contract_last(left, right):
    return lax.dot_general(
        left, right, (((1,), (1,)), ((), ())), preferred_element_type=jnp.float32
    )


def on_device(
    tokens,
    expert_route,
    route_gate,
    request_lengths,
    request_adapter,
    request_order,
    gate_weight,
    up_weight,
    down_weight,
    adapter_in,
    adapter_out,
):
    tok_rows, local_feat = tokens.shape
    groups = lax.axis_size("expert")
    n_mp = lax.axis_size("mp")
    capacity = 4 * tok_rows // groups
    total_slots = groups * capacity
    source_group = lax.axis_index("expert")

    rank_w = adapter_in[0]
    rank_rows_w = rank_w.shape[0]
    both_w = jnp.concatenate([rank_w, down_weight[0]], axis=0)
    both_cols = lax.all_to_all(both_w, "mp", split_axis=1, concat_axis=0, tiled=True).reshape(
        n_mp, both_w.shape[0], local_feat
    )
    rank_cols_w = both_cols[:, :rank_rows_w].reshape(n_mp * rank_rows_w, local_feat)
    down_cols_w = both_cols[:, rank_rows_w:].reshape(-1, local_feat)

    adapter_of = token_adapters(
        request_lengths, request_adapter, request_order, source_group * tok_rows, tok_rows
    )
    slot_index = expert_slots(expert_route, groups, capacity)
    slot_ids = jnp.arange(total_slots, dtype=jnp.int32)[:, None]
    seat = (
        (slot_index[None, :, 0] == slot_ids) | (slot_index[None, :, 1] == slot_ids)
    ).astype(tokens.dtype)
    send_rows = jnp.dot(seat, tokens, preferred_element_type=jnp.float32).astype(tokens.dtype)
    id_plus = jnp.dot(
        seat, (adapter_of + 1).astype(tokens.dtype), preferred_element_type=jnp.float32
    ) - 1.0
    payload = jnp.concatenate(
        [
            send_rows.reshape(groups, capacity, local_feat),
            id_plus.astype(tokens.dtype).reshape(groups, capacity // local_feat, local_feat),
        ],
        axis=1,
    )
    chunk = payload.shape[1]
    received = lax.all_to_all(
        payload.reshape(groups * chunk, local_feat), "expert", split_axis=0, concat_axis=0, tiled=True
    ).reshape(groups, chunk, local_feat)
    arrived_local = received[:, :capacity].reshape(total_slots, local_feat)
    arrived_adapter = received[:, capacity:].reshape(total_slots).astype(jnp.int32)
    row_count = arrived_local.shape[0]

    part_all = contract_last(arrived_local, rank_cols_w)
    pick = (arrived_adapter[:, None] == jnp.arange(ADAPTERS, dtype=jnp.int32)[None, :]).astype(
        jnp.float32
    )
    part_rank = jnp.sum(part_all.reshape(row_count, ADAPTERS, RANK) * pick[:, :, None], axis=1)
    part_rows = row_count * RANK // local_feat
    payload2 = jnp.concatenate(
        [arrived_local, part_rank.astype(tokens.dtype).reshape(part_rows, local_feat)], axis=0
    )
    gathered = lax.all_gather(payload2, "mp", axis=1, tiled=True)
    arrived = gathered[:row_count]
    rank = (
        jnp.sum(
            gathered[row_count:].reshape(part_rows, n_mp, local_feat).astype(jnp.float32), axis=1
        )
        .reshape(row_count, RANK)
        .astype(jnp.bfloat16)
    )

    gate_pre = contract_last(arrived, gate_weight[0])
    up_base = contract_last(arrived, up_weight[0])
    chosen = pick.astype(jnp.bfloat16)
    expanded = (rank[:, None, :] * chosen[:, :, None]).reshape(row_count, ADAPTERS * RANK)
    up = up_base + contract_last(expanded, adapter_out[0])
    hidden = (jax.nn.silu(gate_pre) * up).astype(jnp.bfloat16)
    hidden_full = lax.all_gather(hidden, "mp", axis=1, tiled=True)
    down_local = jnp.dot(hidden_full, down_cols_w, preferred_element_type=jnp.float32).astype(
        jnp.bfloat16
    )
    returned_rows = lax.all_to_all(down_local, "expert", split_axis=0, concat_axis=0, tiled=True)
    picked = returned_rows[slot_index].astype(jnp.float32)
    mixed = jnp.sum(route_gate[:, :, None] * picked, axis=1)
    return mixed.astype(jnp.bfloat16)


def solution(mesh):
    in_specs = (
        P("expert", "mp"),
        P("expert", None),
        P("expert", None),
        P(),
        P(),
        P(),
        P("expert", "mp", None),
        P("expert", "mp", None),
        P("expert", "mp", None),
        P("expert", "mp", None),
        P("expert", "mp", None),
    )
    out_specs = P("expert", "mp")
    return jax.shard_map(
        on_device, mesh=mesh, in_specs=in_specs, out_specs=out_specs, check_vma=False
    )
```

```python
import jax
import jax.numpy as jnp
from jax import lax
from jax.sharding import PartitionSpec as P

RANK = 16
ADAPTERS = 64


def token_adapters(request_lengths, request_adapter, request_order, first_token, token_count):
    request_ids = jnp.arange(request_lengths.shape[0], dtype=jnp.int32)
    chosen = (request_order[:, None] == request_ids[None, :]).astype(jnp.int32)
    packed_lengths = jnp.sum(chosen * request_lengths[None, :], axis=1, dtype=jnp.int32)
    packed_adapters = jnp.sum(chosen * request_adapter[None, :], axis=1, dtype=jnp.int32)
    boundary = jnp.cumsum(packed_lengths, dtype=jnp.int32)
    positions = first_token + jnp.arange(token_count, dtype=jnp.int32)
    packed_index = jnp.sum(
        (boundary[None, :] <= positions[:, None]).astype(jnp.int32), axis=1, dtype=jnp.int32
    )
    matches = (packed_index[:, None] == request_ids[None, :]).astype(jnp.int32)
    return jnp.sum(matches * packed_adapters[None, :], axis=1, dtype=jnp.int32)


def expert_slots(routes, groups, capacity):
    flat_routes = routes.reshape(-1)
    one_hot = (flat_routes[:, None] == jnp.arange(groups, dtype=jnp.int32)[None, :]).astype(
        jnp.int32
    )
    before = jnp.cumsum(one_hot, axis=0, dtype=jnp.int32) - one_hot
    seat_index = jnp.sum(before * one_hot, axis=1, dtype=jnp.int32)
    return (flat_routes * capacity + seat_index).reshape(routes.shape)


def contract_last(left, right):
    return lax.dot_general(
        left, right, (((1,), (1,)), ((), ())), preferred_element_type=jnp.float32
    )


def on_device(
    tokens,
    expert_route,
    route_gate,
    request_lengths,
    request_adapter,
    request_order,
    gate_weight,
    up_weight,
    down_weight,
    adapter_in,
    adapter_out,
):
    tok_rows, local_feat = tokens.shape
    groups = lax.axis_size("expert")
    n_mp = lax.axis_size("mp")
    capacity = 4 * tok_rows // groups
    total_slots = groups * capacity
    source_group = lax.axis_index("expert")

    rank_w = adapter_in[0]
    rank_cols_w = lax.all_to_all(rank_w, "mp", split_axis=1, concat_axis=0, tiled=True)
    down_cols_w = lax.all_to_all(down_weight[0], "mp", split_axis=1, concat_axis=0, tiled=True)

    adapter_of = token_adapters(
        request_lengths, request_adapter, request_order, source_group * tok_rows, tok_rows
    )
    slot_index = expert_slots(expert_route, groups, capacity)
    slot_ids = jnp.arange(total_slots, dtype=jnp.int32)[:, None]
    seat = (
        (slot_index[None, :, 0] == slot_ids) | (slot_index[None, :, 1] == slot_ids)
    ).astype(tokens.dtype)
    send_rows = jnp.dot(seat, tokens, preferred_element_type=jnp.float32).astype(tokens.dtype)
    id_plus = jnp.dot(
        seat, (adapter_of + 1).astype(tokens.dtype), preferred_element_type=jnp.float32
    ) - 1.0
    payload = jnp.concatenate(
        [
            send_rows.reshape(groups, capacity, local_feat),
            id_plus.astype(tokens.dtype).reshape(groups, capacity // local_feat, local_feat),
        ],
        axis=1,
    )
    chunk = payload.shape[1]
    shifted = [lax.dynamic_index_in_dim(payload, source_group, 0, keepdims=False)]
    for shift in range(1, groups):
        sent = lax.dynamic_index_in_dim(payload, (source_group + shift) % groups, 0, keepdims=False)
        pairs = [(i, (i + shift) % groups) for i in range(groups)]
        shifted.append(lax.ppermute(sent, "expert", pairs))
    received = jnp.stack(shifted)
    arrived_local = received[:, :capacity].reshape(total_slots, local_feat)
    arrived_adapter = received[:, capacity:].reshape(total_slots).astype(jnp.int32)
    row_count = arrived_local.shape[0]

    part_all = contract_last(arrived_local, rank_cols_w)
    pick = (arrived_adapter[:, None] == jnp.arange(ADAPTERS, dtype=jnp.int32)[None, :]).astype(
        jnp.float32
    )
    part_rank = jnp.sum(part_all.reshape(row_count, ADAPTERS, RANK) * pick[:, :, None], axis=1)
    part_rows = row_count * RANK // local_feat
    payload2 = jnp.concatenate(
        [arrived_local, part_rank.astype(tokens.dtype).reshape(part_rows, local_feat)], axis=0
    )
    gathered = lax.all_gather(payload2, "mp", axis=1, tiled=True)
    arrived = gathered[:row_count]
    rank = (
        jnp.sum(
            gathered[row_count:].reshape(part_rows, n_mp, local_feat).astype(jnp.float32), axis=1
        )
        .reshape(row_count, RANK)
        .astype(jnp.bfloat16)
    )

    gate_pre = contract_last(arrived, gate_weight[0])
    up_base = contract_last(arrived, up_weight[0])
    chosen = pick.astype(jnp.bfloat16)
    expanded = (rank[:, None, :] * chosen[:, :, None]).reshape(row_count, ADAPTERS * RANK)
    up = up_base + contract_last(expanded, adapter_out[0])
    hidden = (jax.nn.silu(gate_pre) * up).astype(jnp.bfloat16)
    hidden_full = lax.all_gather(hidden, "mp", axis=1, tiled=True)
    down_local = jnp.dot(hidden_full, down_cols_w, preferred_element_type=jnp.float32).astype(
        jnp.bfloat16
    )
    back = down_local.reshape(groups, capacity, local_feat)
    returned = [back[0]]
    for shift in range(1, groups):
        pairs = [(i, (i - shift) % groups) for i in range(groups)]
        returned.append(lax.ppermute(back[shift], "expert", pairs))
    returned_rows = jnp.stack(returned).reshape(total_slots, local_feat)
    route_shift = (expert_route - source_group) % groups
    local_slot = route_shift * capacity + (slot_index - expert_route * capacity)
    picked = returned_rows[local_slot].astype(jnp.float32)
    mixed = jnp.sum(route_gate[:, :, None] * picked, axis=1)
    return mixed.astype(jnp.bfloat16)


def solution(mesh):
    in_specs = (
        P("expert", "mp"),
        P("expert", None),
        P("expert", None),
        P(),
        P(),
        P(),
        P("expert", "mp", None),
        P("expert", "mp", None),
        P("expert", "mp", None),
        P("expert", "mp", None),
        P("expert", "mp", None),
    )
    out_specs = P("expert", "mp")
    return jax.shard_map(
        on_device, mesh=mesh, in_specs=in_specs, out_specs=out_specs, check_vma=False
    )
```

```python
import jax
import jax.numpy as jnp
from jax import lax
from jax.sharding import PartitionSpec as P

RANK = 16
ADAPTERS = 64
USED = 16


def token_adapters(request_lengths, request_adapter, request_order, first_token, token_count):
    request_ids = jnp.arange(request_lengths.shape[0], dtype=jnp.int32)
    chosen = (request_order[:, None] == request_ids[None, :]).astype(jnp.int32)
    packed_lengths = jnp.sum(chosen * request_lengths[None, :], axis=1, dtype=jnp.int32)
    packed_adapters = jnp.sum(chosen * request_adapter[None, :], axis=1, dtype=jnp.int32)
    boundary = jnp.cumsum(packed_lengths, dtype=jnp.int32)
    positions = first_token + jnp.arange(token_count, dtype=jnp.int32)
    packed_index = jnp.sum(
        (boundary[None, :] <= positions[:, None]).astype(jnp.int32), axis=1, dtype=jnp.int32
    )
    matches = (packed_index[:, None] == request_ids[None, :]).astype(jnp.int32)
    return jnp.sum(matches * packed_adapters[None, :], axis=1, dtype=jnp.int32)


def expert_slots(routes, groups, capacity):
    flat_routes = routes.reshape(-1)
    one_hot = (flat_routes[:, None] == jnp.arange(groups, dtype=jnp.int32)[None, :]).astype(
        jnp.int32
    )
    before = jnp.cumsum(one_hot, axis=0, dtype=jnp.int32) - one_hot
    seat_index = jnp.sum(before * one_hot, axis=1, dtype=jnp.int32)
    return (flat_routes * capacity + seat_index).reshape(routes.shape)


def contract_last(left, right):
    return lax.dot_general(
        left, right, (((1,), (1,)), ((), ())), preferred_element_type=jnp.float32
    )


def on_device(
    tokens,
    expert_route,
    route_gate,
    request_lengths,
    request_adapter,
    request_order,
    gate_weight,
    up_weight,
    down_weight,
    adapter_in,
    adapter_out,
):
    tok_rows, local_feat = tokens.shape
    groups = lax.axis_size("expert")
    n_mp = lax.axis_size("mp")
    capacity = 4 * tok_rows // groups
    total_slots = groups * capacity
    source_group = lax.axis_index("expert")

    down_cols_w = lax.all_to_all(down_weight[0], "mp", split_axis=1, concat_axis=0, tiled=True)

    adapter_of = token_adapters(
        request_lengths, request_adapter, request_order, source_group * tok_rows, tok_rows
    )
    slot_index = expert_slots(expert_route, groups, capacity)
    slot_ids = jnp.arange(total_slots, dtype=jnp.int32)[:, None]
    seat = (
        (slot_index[None, :, 0] == slot_ids) | (slot_index[None, :, 1] == slot_ids)
    ).astype(tokens.dtype)
    send_rows = jnp.dot(seat, tokens, preferred_element_type=jnp.float32).astype(tokens.dtype)
    id_plus = jnp.dot(
        seat, (adapter_of + 1).astype(tokens.dtype), preferred_element_type=jnp.float32
    ) - 1.0
    payload = jnp.concatenate(
        [
            send_rows.reshape(groups, capacity, local_feat),
            id_plus.astype(tokens.dtype).reshape(groups, capacity // local_feat, local_feat),
        ],
        axis=1,
    )
    chunk = payload.shape[1]
    received = lax.all_to_all(
        payload.reshape(groups * chunk, local_feat), "expert", split_axis=0, concat_axis=0, tiled=True
    ).reshape(groups, chunk, local_feat)
    arrived_local = received[:, :capacity].reshape(total_slots, local_feat)
    arrived_adapter = received[:, capacity:].reshape(total_slots).astype(jnp.int32)
    row_count = arrived_local.shape[0]

    rank_w = adapter_in[0]
    payload2 = jnp.concatenate([jnp.transpose(arrived_local), rank_w], axis=0)
    gathered = lax.all_gather(payload2, "mp", axis=0, tiled=False)
    arrived_t = gathered[:, :local_feat].reshape(n_mp * local_feat, row_count)
    rank_all_w = gathered[:, local_feat:].reshape(ADAPTERS, RANK, -1)

    adapter_ids = jnp.arange(ADAPTERS, dtype=jnp.int32)
    present = jnp.any(request_adapter[:, None] == adapter_ids[None, :], axis=0)
    order = jnp.cumsum(present.astype(jnp.int32)) - 1
    used_count = USED
    used_pick = (
        present[None, :] & (order[None, :] == jnp.arange(used_count, dtype=jnp.int32)[:, None])
    ).astype(tokens.dtype)
    used_w = jnp.einsum(
        "ia,akf->ikf", used_pick, rank_all_w, preferred_element_type=jnp.float32
    ).astype(tokens.dtype).reshape(used_count * RANK, -1)
    rank_used = lax.dot_general(
        arrived_t, used_w, (((0,), (1,)), ((), ())), preferred_element_type=jnp.float32
    )
    slot_order = jnp.where(arrived_adapter >= 0, order[jnp.clip(arrived_adapter, 0, ADAPTERS - 1)], -1)
    slot_pick = (slot_order[:, None] == jnp.arange(used_count, dtype=jnp.int32)[None, :]).astype(
        jnp.float32
    )
    rank = jnp.sum(
        rank_used.reshape(row_count, used_count, RANK) * slot_pick[:, :, None], axis=1
    ).astype(jnp.bfloat16)

    gate_pre = jnp.dot(gate_weight[0], arrived_t, preferred_element_type=jnp.float32)
    up_base = jnp.dot(up_weight[0], arrived_t, preferred_element_type=jnp.float32)
    chosen = (arrived_adapter[:, None] == adapter_ids[None, :]).astype(jnp.bfloat16)
    expanded = (rank[:, None, :] * chosen[:, :, None]).reshape(row_count, ADAPTERS * RANK)
    up = up_base + contract_last(adapter_out[0], expanded)
    hidden = (jax.nn.silu(gate_pre) * up).astype(jnp.bfloat16)
    hidden_full = lax.all_gather(hidden, "mp", axis=0, tiled=True)
    down_local = lax.dot_general(
        hidden_full, down_cols_w, (((0,), (0,)), ((), ())), preferred_element_type=jnp.float32
    ).astype(jnp.bfloat16)
    returned_rows = lax.all_to_all(down_local, "expert", split_axis=0, concat_axis=0, tiled=True)
    picked = returned_rows[slot_index].astype(jnp.float32)
    mixed = jnp.sum(route_gate[:, :, None] * picked, axis=1)
    return mixed.astype(jnp.bfloat16)


def solution(mesh):
    in_specs = (
        P("expert", "mp"),
        P("expert", None),
        P("expert", None),
        P(),
        P(),
        P(),
        P("expert", "mp", None),
        P("expert", "mp", None),
        P("expert", "mp", None),
        P("expert", "mp", None),
        P("expert", "mp", None),
    )
    out_specs = P("expert", "mp")
    return jax.shard_map(
        on_device, mesh=mesh, in_specs=in_specs, out_specs=out_specs, check_vma=False
    )
```

```python
import jax
import jax.numpy as jnp
from jax import lax
from jax.sharding import PartitionSpec as P

RANK = 16
ADAPTERS = 64
USED = 16


def token_adapters(request_lengths, request_adapter, request_order, first_token, token_count):
    request_ids = jnp.arange(request_lengths.shape[0], dtype=jnp.int32)
    chosen = (request_order[:, None] == request_ids[None, :]).astype(jnp.int32)
    packed_lengths = jnp.sum(chosen * request_lengths[None, :], axis=1, dtype=jnp.int32)
    packed_adapters = jnp.sum(chosen * request_adapter[None, :], axis=1, dtype=jnp.int32)
    boundary = jnp.cumsum(packed_lengths, dtype=jnp.int32)
    positions = first_token + jnp.arange(token_count, dtype=jnp.int32)
    packed_index = jnp.sum(
        (boundary[None, :] <= positions[:, None]).astype(jnp.int32), axis=1, dtype=jnp.int32
    )
    matches = (packed_index[:, None] == request_ids[None, :]).astype(jnp.int32)
    return jnp.sum(matches * packed_adapters[None, :], axis=1, dtype=jnp.int32)


def expert_slots(routes, groups, capacity):
    flat_routes = routes.reshape(-1)
    one_hot = (flat_routes[:, None] == jnp.arange(groups, dtype=jnp.int32)[None, :]).astype(
        jnp.int32
    )
    before = jnp.cumsum(one_hot, axis=0, dtype=jnp.int32) - one_hot
    seat_index = jnp.sum(before * one_hot, axis=1, dtype=jnp.int32)
    return (flat_routes * capacity + seat_index).reshape(routes.shape)


def contract_last(left, right):
    return lax.dot_general(
        left, right, (((1,), (1,)), ((), ())), preferred_element_type=jnp.float32
    )


def on_device(
    tokens,
    expert_route,
    route_gate,
    request_lengths,
    request_adapter,
    request_order,
    gate_weight,
    up_weight,
    down_weight,
    adapter_in,
    adapter_out,
):
    tok_rows, local_feat = tokens.shape
    groups = lax.axis_size("expert")
    n_mp = lax.axis_size("mp")
    capacity = 4 * tok_rows // groups
    total_slots = groups * capacity
    source_group = lax.axis_index("expert")

    down_cols_w = lax.all_to_all(down_weight[0], "mp", split_axis=1, concat_axis=0, tiled=True)

    adapter_of = token_adapters(
        request_lengths, request_adapter, request_order, source_group * tok_rows, tok_rows
    )
    slot_index = expert_slots(expert_route, groups, capacity)
    slot_ids = jnp.arange(total_slots, dtype=jnp.int32)[:, None]
    seat = (
        (slot_index[None, :, 0] == slot_ids) | (slot_index[None, :, 1] == slot_ids)
    ).astype(tokens.dtype)
    send_rows = jnp.dot(seat, tokens, preferred_element_type=jnp.float32).astype(tokens.dtype)
    id_plus = jnp.dot(
        seat, (adapter_of + 1).astype(tokens.dtype), preferred_element_type=jnp.float32
    ) - 1.0
    payload = jnp.concatenate(
        [
            send_rows.reshape(groups, capacity, local_feat),
            id_plus.astype(tokens.dtype).reshape(groups, capacity // local_feat, local_feat),
        ],
        axis=1,
    )
    chunk = payload.shape[1]
    received = lax.all_to_all(
        payload.reshape(groups * chunk, local_feat), "expert", split_axis=0, concat_axis=0, tiled=True
    ).reshape(groups, chunk, local_feat)
    arrived_local = received[:, :capacity].reshape(total_slots, local_feat)
    arrived_adapter = received[:, capacity:].reshape(total_slots).astype(jnp.int32)
    row_count = arrived_local.shape[0]

    rank_w = adapter_in[0]
    payload2 = jnp.concatenate([jnp.transpose(arrived_local), rank_w], axis=0)
    gathered = lax.all_gather(payload2, "mp", axis=0, tiled=False)
    block = gathered.shape[1]
    flat = gathered.reshape(n_mp * block, row_count)
    pad = block - local_feat

    def padded(w):
        lead = w.shape[0]
        return jnp.concatenate(
            [w.reshape(lead, n_mp, local_feat), jnp.zeros((lead, n_mp, pad), w.dtype)], axis=2
        ).reshape(lead, n_mp * block)

    adapter_ids = jnp.arange(ADAPTERS, dtype=jnp.int32)
    present = jnp.any(request_adapter[:, None] == adapter_ids[None, :], axis=0)
    order = jnp.cumsum(present.astype(jnp.int32)) - 1
    used_pick = (
        present[None, :] & (order[None, :] == jnp.arange(USED, dtype=jnp.int32)[:, None])
    ).astype(tokens.dtype)
    groups_per_block = block // RANK
    first_adapter_group = local_feat // RANK
    sel = jnp.concatenate(
        [
            jnp.zeros((USED, n_mp, first_adapter_group), tokens.dtype),
            used_pick.reshape(USED, n_mp, groups_per_block - first_adapter_group),
        ],
        axis=2,
    )
    used_w = jnp.einsum(
        "ijg,jgkf->ikf",
        sel,
        gathered.reshape(n_mp, groups_per_block, RANK, row_count),
        preferred_element_type=jnp.float32,
    ).astype(tokens.dtype).reshape(USED * RANK, -1)
    rank_used = lax.dot_general(
        flat, padded(used_w), (((0,), (1,)), ((), ())), preferred_element_type=jnp.float32
    )
    chosen = (arrived_adapter[:, None] == adapter_ids[None, :]).astype(jnp.bfloat16)
    slot_pick = lax.dot_general(
        chosen, used_pick, (((1,), (1,)), ((), ())), preferred_element_type=jnp.float32
    )
    rank = jnp.sum(
        rank_used.reshape(row_count, USED, RANK) * slot_pick[:, :, None], axis=1
    ).astype(jnp.bfloat16)

    gate_pre = jnp.dot(padded(gate_weight[0]), flat, preferred_element_type=jnp.float32)
    up_base = jnp.dot(padded(up_weight[0]), flat, preferred_element_type=jnp.float32)
    expanded = (rank[:, None, :] * chosen[:, :, None]).reshape(row_count, ADAPTERS * RANK)
    up = up_base + contract_last(adapter_out[0], expanded)
    hidden = (jax.nn.silu(gate_pre) * up).astype(jnp.bfloat16)
    hidden_full = lax.all_gather(hidden, "mp", axis=0, tiled=True)
    down_local = lax.dot_general(
        hidden_full, down_cols_w, (((0,), (0,)), ((), ())), preferred_element_type=jnp.float32
    ).astype(jnp.bfloat16)
    returned_rows = lax.all_to_all(down_local, "expert", split_axis=0, concat_axis=0, tiled=True)
    picked = returned_rows[slot_index].astype(jnp.float32)
    mixed = jnp.sum(route_gate[:, :, None] * picked, axis=1)
    return mixed.astype(jnp.bfloat16)


def solution(mesh):
    in_specs = (
        P("expert", "mp"),
        P("expert", None),
        P("expert", None),
        P(),
        P(),
        P(),
        P("expert", "mp", None),
        P("expert", "mp", None),
        P("expert", "mp", None),
        P("expert", "mp", None),
        P("expert", "mp", None),
    )
    out_specs = P("expert", "mp")
    return jax.shard_map(
        on_device, mesh=mesh, in_specs=in_specs, out_specs=out_specs, check_vma=False
    )
```

```python
import jax
import jax.numpy as jnp
from jax import lax
from jax.sharding import PartitionSpec as P

RANK = 16
ADAPTERS = 64


def token_adapters(request_lengths, request_adapter, request_order, first_token, token_count):
    request_ids = jnp.arange(request_lengths.shape[0], dtype=jnp.int32)
    chosen = (request_order[:, None] == request_ids[None, :]).astype(jnp.int32)
    packed_lengths = jnp.sum(chosen * request_lengths[None, :], axis=1, dtype=jnp.int32)
    packed_adapters = jnp.sum(chosen * request_adapter[None, :], axis=1, dtype=jnp.int32)
    boundary = jnp.cumsum(packed_lengths, dtype=jnp.int32)
    positions = first_token + jnp.arange(token_count, dtype=jnp.int32)
    packed_index = jnp.sum(
        (boundary[None, :] <= positions[:, None]).astype(jnp.int32), axis=1, dtype=jnp.int32
    )
    matches = (packed_index[:, None] == request_ids[None, :]).astype(jnp.int32)
    return jnp.sum(matches * packed_adapters[None, :], axis=1, dtype=jnp.int32)


def expert_slots(routes, groups, capacity):
    flat_routes = routes.reshape(-1)
    one_hot = (flat_routes[:, None] == jnp.arange(groups, dtype=jnp.int32)[None, :]).astype(
        jnp.int32
    )
    before = jnp.cumsum(one_hot, axis=0, dtype=jnp.int32) - one_hot
    seat_index = jnp.sum(before * one_hot, axis=1, dtype=jnp.int32)
    return (flat_routes * capacity + seat_index).reshape(routes.shape)


def contract_last(left, right):
    return lax.dot_general(
        left, right, (((1,), (1,)), ((), ())), preferred_element_type=jnp.float32
    )


def on_device(
    tokens,
    expert_route,
    route_gate,
    request_lengths,
    request_adapter,
    request_order,
    gate_weight,
    up_weight,
    down_weight,
    adapter_in,
    adapter_out,
):
    tok_rows, local_feat = tokens.shape
    groups = lax.axis_size("expert")
    n_mp = lax.axis_size("mp")
    capacity = 4 * tok_rows // groups
    total_slots = groups * capacity
    source_group = lax.axis_index("expert")

    rank_w = adapter_in[0]
    rank_cols_w = lax.all_to_all(rank_w, "mp", split_axis=1, concat_axis=0, tiled=True)
    down_cols_w = lax.all_to_all(down_weight[0], "mp", split_axis=1, concat_axis=0, tiled=True)

    adapter_of = token_adapters(
        request_lengths, request_adapter, request_order, source_group * tok_rows, tok_rows
    )
    slot_index = expert_slots(expert_route, groups, capacity)
    slot_ids = jnp.arange(total_slots, dtype=jnp.int32)[:, None]
    seat = (
        (slot_index[None, :, 0] == slot_ids) | (slot_index[None, :, 1] == slot_ids)
    ).astype(tokens.dtype)
    send_rows = jnp.dot(seat, tokens, preferred_element_type=jnp.float32).astype(tokens.dtype)
    id_plus = jnp.dot(
        seat, (adapter_of + 1).astype(tokens.dtype), preferred_element_type=jnp.float32
    ) - 1.0
    payload = jnp.concatenate(
        [
            send_rows.reshape(groups, capacity, local_feat),
            id_plus.astype(tokens.dtype).reshape(groups, capacity // local_feat, local_feat),
        ],
        axis=1,
    )
    chunk = payload.shape[1]
    shifted = [lax.dynamic_index_in_dim(payload, source_group, 0, keepdims=False)]
    for shift in range(1, groups):
        sent = lax.dynamic_index_in_dim(payload, (source_group + shift) % groups, 0, keepdims=False)
        pairs = [(i, (i + shift) % groups) for i in range(groups)]
        shifted.append(lax.ppermute(sent, "expert", pairs))
    received = jnp.stack(shifted)
    arrived_local = received[:, :capacity].reshape(total_slots, local_feat)
    arrived_adapter = received[:, capacity:].reshape(total_slots).astype(jnp.int32)
    row_count = arrived_local.shape[0]

    part_all = contract_last(arrived_local, rank_cols_w)
    pick = (arrived_adapter[:, None] == jnp.arange(ADAPTERS, dtype=jnp.int32)[None, :]).astype(
        jnp.float32
    )
    part_rank = jnp.sum(part_all.reshape(row_count, ADAPTERS, RANK) * pick[:, :, None], axis=1)
    part_rows = row_count * RANK // local_feat
    payload2 = jnp.concatenate(
        [arrived_local, part_rank.astype(tokens.dtype).reshape(part_rows, local_feat)], axis=0
    )
    gathered = lax.all_gather(payload2, "mp", axis=1, tiled=True)
    arrived = gathered[:row_count]
    rank = (
        jnp.sum(
            gathered[row_count:].reshape(part_rows, n_mp, local_feat).astype(jnp.float32), axis=1
        )
        .reshape(row_count, RANK)
        .astype(jnp.bfloat16)
    )

    gate_pre = contract_last(arrived, gate_weight[0])
    up_base = contract_last(arrived, up_weight[0])
    chosen = pick.astype(jnp.bfloat16)
    expanded = (rank[:, None, :] * chosen[:, :, None]).reshape(row_count, ADAPTERS * RANK)
    up = up_base + contract_last(expanded, adapter_out[0])
    hidden = (jax.nn.silu(gate_pre) * up).astype(jnp.bfloat16)
    hidden_full = lax.all_gather(hidden, "mp", axis=1, tiled=True)
    def down_chunk(shift):
        rows = hidden_full[shift * capacity : (shift + 1) * capacity]
        return jnp.dot(rows, down_cols_w, preferred_element_type=jnp.float32).astype(jnp.bfloat16)

    returned = [down_chunk(0)]
    for shift in range(1, groups):
        pairs = [(i, (i - shift) % groups) for i in range(groups)]
        returned.append(lax.ppermute(down_chunk(shift), "expert", pairs))
    returned_rows = jnp.stack(returned).reshape(total_slots, local_feat)
    route_shift = (expert_route - source_group) % groups
    local_slot = route_shift * capacity + (slot_index - expert_route * capacity)
    picked = returned_rows[local_slot].astype(jnp.float32)
    mixed = jnp.sum(route_gate[:, :, None] * picked, axis=1)
    return mixed.astype(jnp.bfloat16)


def solution(mesh):
    in_specs = (
        P("expert", "mp"),
        P("expert", None),
        P("expert", None),
        P(),
        P(),
        P(),
        P("expert", "mp", None),
        P("expert", "mp", None),
        P("expert", "mp", None),
        P("expert", "mp", None),
        P("expert", "mp", None),
    )
    out_specs = P("expert", "mp")
    return jax.shard_map(
        on_device, mesh=mesh, in_specs=in_specs, out_specs=out_specs, check_vma=False
    )
```

```python
import jax
import jax.numpy as jnp
from jax import lax
from jax.sharding import PartitionSpec as P

RANK = 16
ADAPTERS = 64


def token_adapters(request_lengths, request_adapter, request_order, first_token, token_count):
    request_ids = jnp.arange(request_lengths.shape[0], dtype=jnp.int32)
    chosen = (request_order[:, None] == request_ids[None, :]).astype(jnp.int32)
    packed_lengths = jnp.sum(chosen * request_lengths[None, :], axis=1, dtype=jnp.int32)
    packed_adapters = jnp.sum(chosen * request_adapter[None, :], axis=1, dtype=jnp.int32)
    boundary = jnp.cumsum(packed_lengths, dtype=jnp.int32)
    positions = first_token + jnp.arange(token_count, dtype=jnp.int32)
    packed_index = jnp.sum(
        (boundary[None, :] <= positions[:, None]).astype(jnp.int32), axis=1, dtype=jnp.int32
    )
    matches = (packed_index[:, None] == request_ids[None, :]).astype(jnp.int32)
    return jnp.sum(matches * packed_adapters[None, :], axis=1, dtype=jnp.int32)


def expert_slots(routes, groups, capacity):
    flat_routes = routes.reshape(-1)
    one_hot = (flat_routes[:, None] == jnp.arange(groups, dtype=jnp.int32)[None, :]).astype(
        jnp.int32
    )
    before = jnp.cumsum(one_hot, axis=0, dtype=jnp.int32) - one_hot
    seat_index = jnp.sum(before * one_hot, axis=1, dtype=jnp.int32)
    return (flat_routes * capacity + seat_index).reshape(routes.shape)


def contract_last(left, right):
    return lax.dot_general(
        left, right, (((1,), (1,)), ((), ())), preferred_element_type=jnp.float32
    )


def on_device(
    tokens,
    expert_route,
    route_gate,
    request_lengths,
    request_adapter,
    request_order,
    gate_weight,
    up_weight,
    down_weight,
    adapter_in,
    adapter_out,
):
    tok_rows, local_feat = tokens.shape
    groups = lax.axis_size("expert")
    n_mp = lax.axis_size("mp")
    capacity = 4 * tok_rows // groups
    total_slots = groups * capacity
    source_group = lax.axis_index("expert")

    rank_w = adapter_in[0]
    rank_cols_w = lax.all_to_all(rank_w, "mp", split_axis=1, concat_axis=0, tiled=True)
    down_cols_w = lax.all_to_all(down_weight[0], "mp", split_axis=1, concat_axis=0, tiled=True)

    adapter_of = token_adapters(
        request_lengths, request_adapter, request_order, source_group * tok_rows, tok_rows
    )
    slot_index = expert_slots(expert_route, groups, capacity)
    slot_ids = jnp.arange(total_slots, dtype=jnp.int32)[:, None]
    seat = (
        (slot_index[None, :, 0] == slot_ids) | (slot_index[None, :, 1] == slot_ids)
    ).astype(tokens.dtype)
    send_rows = jnp.dot(seat, tokens, preferred_element_type=jnp.float32).astype(tokens.dtype)
    id_plus = jnp.dot(
        seat, (adapter_of + 1).astype(tokens.dtype), preferred_element_type=jnp.float32
    ) - 1.0
    payload = jnp.concatenate(
        [
            send_rows.reshape(groups, capacity, local_feat),
            id_plus.astype(tokens.dtype).reshape(groups, capacity // local_feat, local_feat),
        ],
        axis=1,
    )
    chunk = payload.shape[1]
    received = lax.all_to_all(
        payload.reshape(groups * chunk, local_feat), "expert", split_axis=0, concat_axis=0, tiled=True
    ).reshape(groups, chunk, local_feat)
    arrived_local = received[:, :capacity].reshape(total_slots, local_feat)
    arrived_adapter = received[:, capacity:].reshape(total_slots).astype(jnp.int32)
    row_count = arrived_local.shape[0]

    part_all = contract_last(arrived_local, rank_cols_w)
    pick = (arrived_adapter[:, None] == jnp.arange(ADAPTERS, dtype=jnp.int32)[None, :]).astype(
        jnp.float32
    )
    part_rank = jnp.sum(part_all.reshape(row_count, ADAPTERS, RANK) * pick[:, :, None], axis=1)
    part_rows = row_count * RANK // local_feat
    payload2 = jnp.concatenate(
        [arrived_local, part_rank.astype(tokens.dtype).reshape(part_rows, local_feat)], axis=0
    )
    gathered = lax.all_gather(payload2, "mp", axis=1, tiled=True)
    arrived = gathered[:row_count]
    rank = (
        jnp.sum(
            gathered[row_count:].reshape(part_rows, n_mp, local_feat).astype(jnp.float32), axis=1
        )
        .reshape(row_count, RANK)
        .astype(jnp.bfloat16)
    )

    gate_pre = contract_last(arrived, gate_weight[0])
    up_base = contract_last(arrived, up_weight[0])
    chosen = pick.astype(jnp.bfloat16)
    expanded = (rank[:, None, :] * chosen[:, :, None]).reshape(row_count, ADAPTERS * RANK)
    up = up_base + contract_last(expanded, adapter_out[0])
    hidden = (jax.nn.silu(gate_pre) * up).astype(jnp.bfloat16)
    hidden_full = lax.all_gather(hidden, "mp", axis=1, tiled=True)
    down_local = jnp.dot(hidden_full, down_cols_w, preferred_element_type=jnp.float32).astype(
        jnp.bfloat16
    )
    returned_rows = lax.all_to_all(down_local, "expert", split_axis=0, concat_axis=0, tiled=True)
    mixed = jnp.zeros((tok_rows, local_feat), jnp.float32)
    for choice in range(slot_index.shape[1]):
        hit = (slot_index[:, choice][:, None] == slot_ids[:, 0][None, :]).astype(returned_rows.dtype)
        picked = jnp.dot(hit, returned_rows, preferred_element_type=jnp.float32)
        mixed = mixed + route_gate[:, choice][:, None] * picked
    return mixed.astype(jnp.bfloat16)


def solution(mesh):
    in_specs = (
        P("expert", "mp"),
        P("expert", None),
        P("expert", None),
        P(),
        P(),
        P(),
        P("expert", "mp", None),
        P("expert", "mp", None),
        P("expert", "mp", None),
        P("expert", "mp", None),
        P("expert", "mp", None),
    )
    out_specs = P("expert", "mp")
    return jax.shard_map(
        on_device, mesh=mesh, in_specs=in_specs, out_specs=out_specs, check_vma=False
    )
```

```python
import jax
import jax.numpy as jnp
from jax import lax
from jax.sharding import PartitionSpec as P

RANK = 16
ADAPTERS = 64


def token_adapters(request_lengths, request_adapter, request_order, first_token, token_count):
    request_ids = jnp.arange(request_lengths.shape[0], dtype=jnp.int32)
    chosen = (request_order[:, None] == request_ids[None, :]).astype(jnp.int32)
    packed_lengths = jnp.sum(chosen * request_lengths[None, :], axis=1, dtype=jnp.int32)
    packed_adapters = jnp.sum(chosen * request_adapter[None, :], axis=1, dtype=jnp.int32)
    boundary = jnp.cumsum(packed_lengths, dtype=jnp.int32)
    positions = first_token + jnp.arange(token_count, dtype=jnp.int32)
    packed_index = jnp.sum(
        (boundary[None, :] <= positions[:, None]).astype(jnp.int32), axis=1, dtype=jnp.int32
    )
    matches = (packed_index[:, None] == request_ids[None, :]).astype(jnp.int32)
    return jnp.sum(matches * packed_adapters[None, :], axis=1, dtype=jnp.int32)


def expert_slots(routes, groups, capacity):
    flat_routes = routes.reshape(-1)
    one_hot = (flat_routes[:, None] == jnp.arange(groups, dtype=jnp.int32)[None, :]).astype(
        jnp.int32
    )
    before = jnp.cumsum(one_hot, axis=0, dtype=jnp.int32) - one_hot
    seat_index = jnp.sum(before * one_hot, axis=1, dtype=jnp.int32)
    return (flat_routes * capacity + seat_index).reshape(routes.shape)


def contract_last(left, right):
    return lax.dot_general(
        left, right, (((1,), (1,)), ((), ())), preferred_element_type=jnp.float32
    )


def on_device(
    tokens,
    expert_route,
    route_gate,
    request_lengths,
    request_adapter,
    request_order,
    gate_weight,
    up_weight,
    down_weight,
    adapter_in,
    adapter_out,
):
    tok_rows, local_feat = tokens.shape
    groups = lax.axis_size("expert")
    n_mp = lax.axis_size("mp")
    capacity = 4 * tok_rows // groups
    total_slots = groups * capacity
    source_group = lax.axis_index("expert")

    rank_w = adapter_in[0]
    rank_cols_w = lax.all_to_all(rank_w, "mp", split_axis=1, concat_axis=0, tiled=True)
    gate_up_w = jnp.concatenate([gate_weight[0], up_weight[0]], axis=0)
    down_cols_w = lax.all_to_all(down_weight[0], "mp", split_axis=1, concat_axis=0, tiled=True)

    adapter_of = token_adapters(
        request_lengths, request_adapter, request_order, source_group * tok_rows, tok_rows
    )
    slot_index = expert_slots(expert_route, groups, capacity)
    slot_ids = jnp.arange(total_slots, dtype=jnp.int32)[:, None]
    seat = (
        (slot_index[None, :, 0] == slot_ids) | (slot_index[None, :, 1] == slot_ids)
    ).astype(tokens.dtype)
    send_rows = jnp.dot(seat, tokens, preferred_element_type=jnp.float32).astype(tokens.dtype)
    id_plus = jnp.dot(
        seat, (adapter_of + 1).astype(tokens.dtype), preferred_element_type=jnp.float32
    ) - 1.0
    payload = jnp.concatenate(
        [
            send_rows.reshape(groups, capacity, local_feat),
            id_plus.astype(tokens.dtype).reshape(groups, capacity // local_feat, local_feat),
        ],
        axis=1,
    )
    chunk = payload.shape[1]
    received = lax.all_to_all(
        payload.reshape(groups * chunk, local_feat), "expert", split_axis=0, concat_axis=0, tiled=True
    ).reshape(groups, chunk, local_feat)
    arrived_local = received[:, :capacity].reshape(total_slots, local_feat)
    arrived_adapter = received[:, capacity:].reshape(total_slots).astype(jnp.int32)
    row_count = arrived_local.shape[0]

    part_all = contract_last(arrived_local, rank_cols_w)
    pick = (arrived_adapter[:, None] == jnp.arange(ADAPTERS, dtype=jnp.int32)[None, :]).astype(
        jnp.float32
    )
    part_rank = jnp.sum(part_all.reshape(row_count, ADAPTERS, RANK) * pick[:, :, None], axis=1)
    part_rows = row_count * RANK // local_feat
    payload2 = jnp.concatenate(
        [arrived_local, part_rank.astype(tokens.dtype).reshape(part_rows, local_feat)], axis=0
    )
    gathered = lax.all_gather(payload2, "mp", axis=1, tiled=True)
    arrived = gathered[:row_count]
    rank = (
        jnp.sum(
            gathered[row_count:].reshape(part_rows, n_mp, local_feat).astype(jnp.float32), axis=1
        )
        .reshape(row_count, RANK)
        .astype(jnp.bfloat16)
    )

    units = gate_weight.shape[1]
    gate_up = contract_last(arrived, gate_up_w)
    gate_pre = gate_up[:, :units]
    up_base = gate_up[:, units:]
    chosen = pick.astype(jnp.bfloat16)
    expanded = (rank[:, None, :] * chosen[:, :, None]).reshape(row_count, ADAPTERS * RANK)
    up = up_base + contract_last(expanded, adapter_out[0])
    hidden = (jax.nn.silu(gate_pre) * up).astype(jnp.bfloat16)
    hidden_full = lax.all_gather(hidden, "mp", axis=1, tiled=True)
    down_local = jnp.dot(hidden_full, down_cols_w, preferred_element_type=jnp.float32).astype(
        jnp.bfloat16
    )
    returned_rows = lax.all_to_all(down_local, "expert", split_axis=0, concat_axis=0, tiled=True)
    mixed = jnp.zeros((tok_rows, local_feat), jnp.float32)
    for choice in range(slot_index.shape[1]):
        hit = (slot_index[:, choice][:, None] == slot_ids[:, 0][None, :]).astype(returned_rows.dtype)
        picked = jnp.dot(hit, returned_rows, preferred_element_type=jnp.float32)
        mixed = mixed + route_gate[:, choice][:, None] * picked
    return mixed.astype(jnp.bfloat16)


def solution(mesh):
    in_specs = (
        P("expert", "mp"),
        P("expert", None),
        P("expert", None),
        P(),
        P(),
        P(),
        P("expert", "mp", None),
        P("expert", "mp", None),
        P("expert", "mp", None),
        P("expert", "mp", None),
        P("expert", "mp", None),
    )
    out_specs = P("expert", "mp")
    return jax.shard_map(
        on_device, mesh=mesh, in_specs=in_specs, out_specs=out_specs, check_vma=False
    )
```

```python
import jax
import jax.numpy as jnp
from jax import lax
from jax.sharding import PartitionSpec as P

RANK = 16
ADAPTERS = 64


def token_adapters(request_lengths, request_adapter, request_order, first_token, token_count):
    request_ids = jnp.arange(request_lengths.shape[0], dtype=jnp.int32)
    chosen = (request_order[:, None] == request_ids[None, :]).astype(jnp.int32)
    packed_lengths = jnp.sum(chosen * request_lengths[None, :], axis=1, dtype=jnp.int32)
    packed_adapters = jnp.sum(chosen * request_adapter[None, :], axis=1, dtype=jnp.int32)
    boundary = jnp.cumsum(packed_lengths, dtype=jnp.int32)
    positions = first_token + jnp.arange(token_count, dtype=jnp.int32)
    packed_index = jnp.sum(
        (boundary[None, :] <= positions[:, None]).astype(jnp.int32), axis=1, dtype=jnp.int32
    )
    matches = (packed_index[:, None] == request_ids[None, :]).astype(jnp.int32)
    return jnp.sum(matches * packed_adapters[None, :], axis=1, dtype=jnp.int32)


def expert_slots(routes, groups, capacity):
    flat_routes = routes.reshape(-1)
    one_hot = (flat_routes[:, None] == jnp.arange(groups, dtype=jnp.int32)[None, :]).astype(
        jnp.int32
    )
    count = flat_routes.shape[0]
    earlier = (
        jnp.arange(count, dtype=jnp.int32)[None, :] < jnp.arange(count, dtype=jnp.int32)[:, None]
    ).astype(jnp.bfloat16)
    before = jnp.dot(
        earlier, one_hot.astype(jnp.bfloat16), preferred_element_type=jnp.float32
    ).astype(jnp.int32)
    seat_index = jnp.sum(before * one_hot, axis=1, dtype=jnp.int32)
    return (flat_routes * capacity + seat_index).reshape(routes.shape)


def contract_last(left, right):
    return lax.dot_general(
        left, right, (((1,), (1,)), ((), ())), preferred_element_type=jnp.float32
    )


def on_device(
    tokens,
    expert_route,
    route_gate,
    request_lengths,
    request_adapter,
    request_order,
    gate_weight,
    up_weight,
    down_weight,
    adapter_in,
    adapter_out,
):
    tok_rows, local_feat = tokens.shape
    groups = lax.axis_size("expert")
    n_mp = lax.axis_size("mp")
    capacity = 4 * tok_rows // groups
    total_slots = groups * capacity
    source_group = lax.axis_index("expert")

    rank_w = adapter_in[0]
    rank_cols_w = lax.all_to_all(rank_w, "mp", split_axis=1, concat_axis=0, tiled=True)
    gate_up_w = jnp.concatenate([gate_weight[0], up_weight[0]], axis=0)
    down_cols_w = lax.all_to_all(down_weight[0], "mp", split_axis=1, concat_axis=0, tiled=True)

    adapter_of = token_adapters(
        request_lengths, request_adapter, request_order, source_group * tok_rows, tok_rows
    )
    slot_index = expert_slots(expert_route, groups, capacity)
    slot_ids = jnp.arange(total_slots, dtype=jnp.int32)[:, None]
    seat = (
        (slot_index[None, :, 0] == slot_ids) | (slot_index[None, :, 1] == slot_ids)
    ).astype(tokens.dtype)
    send_rows = jnp.dot(seat, tokens, preferred_element_type=jnp.float32).astype(tokens.dtype)
    id_plus = jnp.dot(
        seat, (adapter_of + 1).astype(tokens.dtype), preferred_element_type=jnp.float32
    ) - 1.0
    payload = jnp.concatenate(
        [
            send_rows.reshape(groups, capacity, local_feat),
            id_plus.astype(tokens.dtype).reshape(groups, capacity // local_feat, local_feat),
        ],
        axis=1,
    )
    chunk = payload.shape[1]
    received = lax.all_to_all(
        payload.reshape(groups * chunk, local_feat), "expert", split_axis=0, concat_axis=0, tiled=True
    ).reshape(groups, chunk, local_feat)
    arrived_local = received[:, :capacity].reshape(total_slots, local_feat)
    arrived_adapter = received[:, capacity:].reshape(total_slots).astype(jnp.int32)
    row_count = arrived_local.shape[0]

    part_all = contract_last(arrived_local, rank_cols_w)
    pick = (arrived_adapter[:, None] == jnp.arange(ADAPTERS, dtype=jnp.int32)[None, :]).astype(
        jnp.float32
    )
    part_rank = jnp.sum(part_all.reshape(row_count, ADAPTERS, RANK) * pick[:, :, None], axis=1)
    part_rows = row_count * RANK // local_feat
    payload2 = jnp.concatenate(
        [arrived_local, part_rank.astype(tokens.dtype).reshape(part_rows, local_feat)], axis=0
    )
    gathered = lax.all_gather(payload2, "mp", axis=1, tiled=True)
    arrived = gathered[:row_count]
    rank = (
        jnp.sum(
            gathered[row_count:].reshape(part_rows, n_mp, local_feat).astype(jnp.float32), axis=1
        )
        .reshape(row_count, RANK)
        .astype(jnp.bfloat16)
    )

    units = gate_weight.shape[1]
    gate_up = contract_last(arrived, gate_up_w)
    gate_pre = gate_up[:, :units]
    up_base = gate_up[:, units:]
    chosen = pick.astype(jnp.bfloat16)
    expanded = (rank[:, None, :] * chosen[:, :, None]).reshape(row_count, ADAPTERS * RANK)
    up = up_base + contract_last(expanded, adapter_out[0])
    hidden = (jax.nn.silu(gate_pre) * up).astype(jnp.bfloat16)
    hidden_full = lax.all_gather(hidden, "mp", axis=1, tiled=True)
    down_local = jnp.dot(hidden_full, down_cols_w, preferred_element_type=jnp.float32).astype(
        jnp.bfloat16
    )
    returned_rows = lax.all_to_all(down_local, "expert", split_axis=0, concat_axis=0, tiled=True)
    mixed = jnp.zeros((tok_rows, local_feat), jnp.float32)
    for choice in range(slot_index.shape[1]):
        hit = (slot_index[:, choice][:, None] == slot_ids[:, 0][None, :]).astype(returned_rows.dtype)
        picked = jnp.dot(hit, returned_rows, preferred_element_type=jnp.float32)
        mixed = mixed + route_gate[:, choice][:, None] * picked
    return mixed.astype(jnp.bfloat16)


def solution(mesh):
    in_specs = (
        P("expert", "mp"),
        P("expert", None),
        P("expert", None),
        P(),
        P(),
        P(),
        P("expert", "mp", None),
        P("expert", "mp", None),
        P("expert", "mp", None),
        P("expert", "mp", None),
        P("expert", "mp", None),
    )
    out_specs = P("expert", "mp")
    return jax.shard_map(
        on_device, mesh=mesh, in_specs=in_specs, out_specs=out_specs, check_vma=False
    )
```

```python
import jax
import jax.numpy as jnp
from jax import lax
from jax.sharding import PartitionSpec as P

RANK = 16
ADAPTERS = 64


def token_adapters(request_lengths, request_adapter, request_order, first_token, token_count):
    request_ids = jnp.arange(request_lengths.shape[0], dtype=jnp.int32)
    chosen = (request_order[:, None] == request_ids[None, :]).astype(jnp.int32)
    packed_lengths = jnp.sum(chosen * request_lengths[None, :], axis=1, dtype=jnp.int32)
    packed_adapters = jnp.sum(chosen * request_adapter[None, :], axis=1, dtype=jnp.int32)
    boundary = jnp.cumsum(packed_lengths, dtype=jnp.int32)
    positions = first_token + jnp.arange(token_count, dtype=jnp.int32)
    packed_index = jnp.sum(
        (boundary[None, :] <= positions[:, None]).astype(jnp.int32), axis=1, dtype=jnp.int32
    )
    matches = (packed_index[:, None] == request_ids[None, :]).astype(jnp.int32)
    return jnp.sum(matches * packed_adapters[None, :], axis=1, dtype=jnp.int32)


def expert_slots(routes, groups, capacity):
    flat_routes = routes.reshape(-1)
    one_hot = (flat_routes[:, None] == jnp.arange(groups, dtype=jnp.int32)[None, :]).astype(
        jnp.int32
    )
    count = flat_routes.shape[0]
    earlier = (
        jnp.arange(count, dtype=jnp.int32)[None, :] < jnp.arange(count, dtype=jnp.int32)[:, None]
    ).astype(jnp.bfloat16)
    before = jnp.dot(
        earlier, one_hot.astype(jnp.bfloat16), preferred_element_type=jnp.float32
    ).astype(jnp.int32)
    seat_index = jnp.sum(before * one_hot, axis=1, dtype=jnp.int32)
    return (flat_routes * capacity + seat_index).reshape(routes.shape)


def contract_last(left, right):
    return lax.dot_general(
        left, right, (((1,), (1,)), ((), ())), preferred_element_type=jnp.float32
    )


def on_device(
    tokens,
    expert_route,
    route_gate,
    request_lengths,
    request_adapter,
    request_order,
    gate_weight,
    up_weight,
    down_weight,
    adapter_in,
    adapter_out,
):
    tok_rows, local_feat = tokens.shape
    groups = lax.axis_size("expert")
    n_mp = lax.axis_size("mp")
    capacity = 4 * tok_rows // groups
    total_slots = groups * capacity
    source_group = lax.axis_index("expert")

    rank_w = adapter_in[0]
    rank_cols_w = lax.all_to_all(rank_w, "mp", split_axis=1, concat_axis=0, tiled=True)
    gate_up_w = jnp.concatenate([gate_weight[0], up_weight[0]], axis=0)
    down_cols_w = lax.all_to_all(down_weight[0], "mp", split_axis=1, concat_axis=0, tiled=True)

    adapter_of = token_adapters(
        request_lengths, request_adapter, request_order, source_group * tok_rows, tok_rows
    )
    slot_index = expert_slots(expert_route, groups, capacity)
    slot_ids = jnp.arange(total_slots, dtype=jnp.int32)[:, None]
    seat = (
        (slot_index[None, :, 0] == slot_ids) | (slot_index[None, :, 1] == slot_ids)
    ).astype(tokens.dtype)
    with_ids = jnp.concatenate([tokens, (adapter_of + 1).astype(tokens.dtype)[:, None]], axis=1)
    seated = jnp.dot(seat, with_ids, preferred_element_type=jnp.float32)
    send_rows = seated[:, :local_feat].astype(tokens.dtype)
    id_plus = seated[:, local_feat] - 1.0
    payload = jnp.concatenate(
        [
            send_rows.reshape(groups, capacity, local_feat),
            id_plus.astype(tokens.dtype).reshape(groups, capacity // local_feat, local_feat),
        ],
        axis=1,
    )
    chunk = payload.shape[1]
    received = lax.all_to_all(
        payload.reshape(groups * chunk, local_feat), "expert", split_axis=0, concat_axis=0, tiled=True
    ).reshape(groups, chunk, local_feat)
    arrived_local = received[:, :capacity].reshape(total_slots, local_feat)
    arrived_adapter = received[:, capacity:].reshape(total_slots).astype(jnp.int32)
    row_count = arrived_local.shape[0]

    part_all = contract_last(arrived_local, rank_cols_w)
    pick = (arrived_adapter[:, None] == jnp.arange(ADAPTERS, dtype=jnp.int32)[None, :]).astype(
        jnp.float32
    )
    part_rank = jnp.sum(part_all.reshape(row_count, ADAPTERS, RANK) * pick[:, :, None], axis=1)
    part_rows = row_count * RANK // local_feat
    payload2 = jnp.concatenate(
        [arrived_local, part_rank.astype(tokens.dtype).reshape(part_rows, local_feat)], axis=0
    )
    gathered = lax.all_gather(payload2, "mp", axis=1, tiled=True)
    arrived = gathered[:row_count]
    rank = (
        jnp.sum(
            gathered[row_count:].reshape(part_rows, n_mp, local_feat).astype(jnp.float32), axis=1
        )
        .reshape(row_count, RANK)
        .astype(jnp.bfloat16)
    )

    units = gate_weight.shape[1]
    gate_up = contract_last(arrived, gate_up_w)
    gate_pre = gate_up[:, :units]
    up_base = gate_up[:, units:]
    chosen = pick.astype(jnp.bfloat16)
    expanded = (rank[:, None, :] * chosen[:, :, None]).reshape(row_count, ADAPTERS * RANK)
    up = up_base + contract_last(expanded, adapter_out[0])
    hidden = (jax.nn.silu(gate_pre) * up).astype(jnp.bfloat16)
    hidden_full = lax.all_gather(hidden, "mp", axis=1, tiled=True)
    down_local = jnp.dot(hidden_full, down_cols_w, preferred_element_type=jnp.float32).astype(
        jnp.bfloat16
    )
    returned_rows = lax.all_to_all(down_local, "expert", split_axis=0, concat_axis=0, tiled=True)
    mixed = jnp.zeros((tok_rows, local_feat), jnp.float32)
    for choice in range(slot_index.shape[1]):
        hit = (slot_index[:, choice][:, None] == slot_ids[:, 0][None, :]).astype(returned_rows.dtype)
        picked = jnp.dot(hit, returned_rows, preferred_element_type=jnp.float32)
        mixed = mixed + route_gate[:, choice][:, None] * picked
    return mixed.astype(jnp.bfloat16)


def solution(mesh):
    in_specs = (
        P("expert", "mp"),
        P("expert", None),
        P("expert", None),
        P(),
        P(),
        P(),
        P("expert", "mp", None),
        P("expert", "mp", None),
        P("expert", "mp", None),
        P("expert", "mp", None),
        P("expert", "mp", None),
    )
    out_specs = P("expert", "mp")
    return jax.shard_map(
        on_device, mesh=mesh, in_specs=in_specs, out_specs=out_specs, check_vma=False
    )
```

```python
import jax
import jax.numpy as jnp
from jax import lax
from jax.sharding import PartitionSpec as P

RANK = 16
ADAPTERS = 64


def token_adapters(request_lengths, request_adapter, request_order, first_token, token_count):
    request_ids = jnp.arange(request_lengths.shape[0], dtype=jnp.int32)
    chosen = (request_order[:, None] == request_ids[None, :]).astype(jnp.int32)
    packed_lengths = jnp.sum(chosen * request_lengths[None, :], axis=1, dtype=jnp.int32)
    packed_adapters = jnp.sum(chosen * request_adapter[None, :], axis=1, dtype=jnp.int32)
    boundary = jnp.cumsum(packed_lengths, dtype=jnp.int32)
    positions = first_token + jnp.arange(token_count, dtype=jnp.int32)
    packed_index = jnp.sum(
        (boundary[None, :] <= positions[:, None]).astype(jnp.int32), axis=1, dtype=jnp.int32
    )
    matches = (packed_index[:, None] == request_ids[None, :]).astype(jnp.int32)
    return jnp.sum(matches * packed_adapters[None, :], axis=1, dtype=jnp.int32)


def expert_slots(routes, groups, capacity):
    flat_routes = routes.reshape(-1)
    one_hot = (flat_routes[:, None] == jnp.arange(groups, dtype=jnp.int32)[None, :]).astype(
        jnp.int32
    )
    count = flat_routes.shape[0]
    earlier = (
        jnp.arange(count, dtype=jnp.int32)[None, :] < jnp.arange(count, dtype=jnp.int32)[:, None]
    ).astype(jnp.bfloat16)
    before = jnp.dot(
        earlier, one_hot.astype(jnp.bfloat16), preferred_element_type=jnp.float32
    ).astype(jnp.int32)
    seat_index = jnp.sum(before * one_hot, axis=1, dtype=jnp.int32)
    return (flat_routes * capacity + seat_index).reshape(routes.shape)


def contract_last(left, right):
    return lax.dot_general(
        left, right, (((1,), (1,)), ((), ())), preferred_element_type=jnp.float32
    )


def on_device(
    tokens,
    expert_route,
    route_gate,
    request_lengths,
    request_adapter,
    request_order,
    gate_weight,
    up_weight,
    down_weight,
    adapter_in,
    adapter_out,
):
    tok_rows, local_feat = tokens.shape
    groups = lax.axis_size("expert")
    n_mp = lax.axis_size("mp")
    capacity = 4 * tok_rows // groups
    total_slots = groups * capacity
    source_group = lax.axis_index("expert")

    gate_up_w = jnp.concatenate([gate_weight[0], up_weight[0]], axis=0)
    down_cols_w = lax.all_to_all(down_weight[0], "mp", split_axis=1, concat_axis=0, tiled=True)

    adapter_of = token_adapters(
        request_lengths, request_adapter, request_order, source_group * tok_rows, tok_rows
    )
    slot_index = expert_slots(expert_route, groups, capacity)
    slot_index, rank_w = lax.optimization_barrier((slot_index, adapter_in[0]))
    rank_cols_w = lax.all_to_all(rank_w, "mp", split_axis=1, concat_axis=0, tiled=True)
    slot_ids = jnp.arange(total_slots, dtype=jnp.int32)[:, None]
    seat = (
        (slot_index[None, :, 0] == slot_ids) | (slot_index[None, :, 1] == slot_ids)
    ).astype(tokens.dtype)
    send_rows = jnp.dot(seat, tokens, preferred_element_type=jnp.float32).astype(tokens.dtype)
    id_plus = jnp.dot(
        seat, (adapter_of + 1).astype(tokens.dtype), preferred_element_type=jnp.float32
    ) - 1.0
    payload = jnp.concatenate(
        [
            send_rows.reshape(groups, capacity, local_feat),
            id_plus.astype(tokens.dtype).reshape(groups, capacity // local_feat, local_feat),
        ],
        axis=1,
    )
    chunk = payload.shape[1]
    received = lax.all_to_all(
        payload.reshape(groups * chunk, local_feat), "expert", split_axis=0, concat_axis=0, tiled=True
    ).reshape(groups, chunk, local_feat)
    arrived_local = received[:, :capacity].reshape(total_slots, local_feat)
    arrived_adapter = received[:, capacity:].reshape(total_slots).astype(jnp.int32)
    row_count = arrived_local.shape[0]

    part_all = contract_last(arrived_local, rank_cols_w)
    pick = (arrived_adapter[:, None] == jnp.arange(ADAPTERS, dtype=jnp.int32)[None, :]).astype(
        jnp.float32
    )
    part_rank = jnp.sum(part_all.reshape(row_count, ADAPTERS, RANK) * pick[:, :, None], axis=1)
    part_rows = row_count * RANK // local_feat
    payload2 = jnp.concatenate(
        [arrived_local, part_rank.astype(tokens.dtype).reshape(part_rows, local_feat)], axis=0
    )
    gathered = lax.all_gather(payload2, "mp", axis=1, tiled=True)
    arrived = gathered[:row_count]
    rank = (
        jnp.sum(
            gathered[row_count:].reshape(part_rows, n_mp, local_feat).astype(jnp.float32), axis=1
        )
        .reshape(row_count, RANK)
        .astype(jnp.bfloat16)
    )

    units = gate_weight.shape[1]
    gate_up = contract_last(arrived, gate_up_w)
    gate_pre = gate_up[:, :units]
    up_base = gate_up[:, units:]
    chosen = pick.astype(jnp.bfloat16)
    expanded = (rank[:, None, :] * chosen[:, :, None]).reshape(row_count, ADAPTERS * RANK)
    up = up_base + contract_last(expanded, adapter_out[0])
    hidden = (jax.nn.silu(gate_pre) * up).astype(jnp.bfloat16)
    hidden_full = lax.all_gather(hidden, "mp", axis=1, tiled=True)
    down_local = jnp.dot(hidden_full, down_cols_w, preferred_element_type=jnp.float32).astype(
        jnp.bfloat16
    )
    returned_rows = lax.all_to_all(down_local, "expert", split_axis=0, concat_axis=0, tiled=True)
    mixed = jnp.zeros((tok_rows, local_feat), jnp.float32)
    for choice in range(slot_index.shape[1]):
        hit = (slot_index[:, choice][:, None] == slot_ids[:, 0][None, :]).astype(returned_rows.dtype)
        picked = jnp.dot(hit, returned_rows, preferred_element_type=jnp.float32)
        mixed = mixed + route_gate[:, choice][:, None] * picked
    return mixed.astype(jnp.bfloat16)


def solution(mesh):
    in_specs = (
        P("expert", "mp"),
        P("expert", None),
        P("expert", None),
        P(),
        P(),
        P(),
        P("expert", "mp", None),
        P("expert", "mp", None),
        P("expert", "mp", None),
        P("expert", "mp", None),
        P("expert", "mp", None),
    )
    out_specs = P("expert", "mp")
    return jax.shard_map(
        on_device, mesh=mesh, in_specs=in_specs, out_specs=out_specs, check_vma=False
    )
```
